1024 devices in a mesh: tm: 128 (over z, y_hi, core), fsdp: 8 (over x, y_lo).
Axes of the slice: x: 4, y: 8 (y_hi: 4, y_lo: 2; y = y_hi * 2 + y_lo), z: 16, core: 2. Of those that a mesh axis runs over, the one named last changes fastest.
Arguments:
- queries: bfloat16 [8, 16384, 768], P('fsdp', 'tm'), may hold values from -135 to 135, as said below
- keys_values: bfloat16 [8, 16384, 1536], P('fsdp', 'tm'), may hold values from -4.5 to 4.5
- inputs: bfloat16 [8, 16384, 1536], P('fsdp', 'tm'), may hold values from -6 to 6
- cotangent: bfloat16 [8, 16384, 1536], P('fsdp', 'tm'), may hold values from -6 to 6
- out_weight: bfloat16 [768, 1536], P('fsdp'), may hold values from -0.21875 to 0.21875
- conv_kernel: bfloat16 [32, 1536], P(None, 'fsdp'), may hold values from -1 to 1
- utt_starts: int32 [8, 16], P('fsdp'), may hold values from 0 to 16383, as said below
Outputs:
- context_grad: bfloat16 [8, 16384, 768], P('fsdp', 'tm')
- weight_grad: float32 [768, 1536], P('fsdp')
- kernel_grad: float32 [32, 1536], P(None, 'fsdp')
The draws below stay inside these ranges and needn't reach their ends.
Inputs may be any that keep to these rules, and one draw needn't show every extreme that they name: In the hidden draw some frames' queries are large multiples of their own keys, so that a few scores are far above the rest. `utt_starts`: each row begins with 0 and rises strictly; entry u is the first frame of utterance u of that packed sequence.
All inputs are finite; a program needn't handle non-finite values.
Results may differ from the reference program's by a relative error of at most 0.014.
Values may be sent and summed in bfloat16 or wider, within the bound.
No kernel may reach another device: no remote copies, remote signals or barrier semaphores. Data moves between devices by JAX's collectives and lax.ppermute only.
A program may use at most 128 MiB of HBM per device.

```python
import math
import jax
import jax.numpy as jnp
from jax import lax

D = 1536
HEADS_W = 8
HD = 96
KW = 32
WIN = 128
UTTS = 16
HW = 768
SEQS = 8
FRAMES = 16384


def attention_pair(key):
    base_key = jax.random.fold_in(key, 11)
    query_key, keyrow_key, value_key = jax.random.split(base_key, 3)
    draw_shape = (SEQS, FRAMES, HW)
    key_draw = jnp.clip(jax.random.normal(keyrow_key, draw_shape, jnp.float32), -4.0, 4.0)
    value_draw = jnp.clip(jax.random.normal(value_key, draw_shape, jnp.float32), -4.0, 4.0)
    query_draw = jnp.clip(jax.random.normal(query_key, draw_shape, jnp.float32), -4.0, 4.0)
    return (query_draw, jnp.concatenate([key_draw, value_draw], axis=2))


def draw_queries(key, part):
    return attention_pair(key)[0].astype(jnp.bfloat16)


def draw_keys_values(key, part):
    return attention_pair(key)[1].astype(jnp.bfloat16)


def draw_utt_starts(key, part):
    base_key = jax.random.fold_in(key, 5)
    row_keys = jax.random.split(base_key, SEQS)

    def one_row(row_key):
        chosen = jax.random.permutation(row_key, FRAMES - 2)[:UTTS - 2] + 1
        inner = jnp.sort(chosen).astype(jnp.int32)
        return jnp.concatenate([jnp.zeros((1,), jnp.int32), inner, jnp.full((1,), FRAMES - 1, jnp.int32)])
    return jax.vmap(one_row)(row_keys)


def level_of(key, dims, cuts, least, top_value):
    level, own = 1.0, jax.random.fold_in(key, 6)
    for position, shards_of in cuts:
        steps = jnp.exp(jax.random.uniform(jax.random.fold_in(own, position), (shards_of,), jnp.float32, least / len(cuts), top_value / len(cuts)))
        level = level * jnp.repeat(steps, dims[position] // shards_of).reshape([-1 if axis == position else 1 for axis in range(len(dims))])
    return level


def normal_values(key, extent, spread, most, cuts=(), kind=jnp.bfloat16):
    loudness = level_of(key, extent, cuts, -0.22, 0.18) if cuts else 1.0
    entries = jax.random.normal(key, extent, jnp.float32) * spread * loudness
    return jnp.minimum(jnp.maximum(entries, -most), most).astype(kind)


def setup_inputs(seed: int = 0) -> dict:
    seeds = jax.random.split(jax.random.key(seed), 8)
    queries = draw_queries(jax.random.fold_in(seeds[7], 71), 0)
    keys_values = draw_keys_values(jax.random.fold_in(seeds[7], 71), 0)
    inputs = normal_values(seeds[2], (SEQS, FRAMES, D), 1.0, 6.0, ((0, 8), (1, 128)))
    cotangent = normal_values(seeds[3], (SEQS, FRAMES, D), 1.0, 6.0, ((0, 8), (1, 128)))
    out_weight = normal_values(seeds[4], (HW, D), HW ** -0.5, 0.21875, ((0, 8),))
    conv_kernel = normal_values(seeds[5], (KW, D), KW ** -0.5, 1.0, ((1, 8),))
    utt_starts = draw_utt_starts(jax.random.fold_in(seeds[7], 71), 0)
    return dict(queries=queries, keys_values=keys_values, inputs=inputs, cotangent=cotangent, out_weight=out_weight, conv_kernel=conv_kernel, utt_starts=utt_starts)


masked_score = -1e+30

def segment_ids(starts_row, positions):
    return lax.optimization_barrier(jnp.sum((starts_row[None, :] <= positions[:, None]).astype(jnp.int32), axis=1)) - 1

def attend_sequence(query_rows, kv_rows, segments):
    window_half = WIN // 2
    padded_kv = jnp.pad(kv_rows, ((window_half, window_half), (0, 0)))
    padded_seg = jnp.pad(segments, (window_half, window_half), constant_values=-1)
    block_rows = min(FRAMES, 512)
    block_count = FRAMES // block_rows
    key_span = block_rows + 2 * window_half
    key_offset = jnp.arange(key_span, dtype=jnp.int32)[None, :] - jnp.arange(block_rows, dtype=jnp.int32)[:, None]
    in_window = (key_offset >= 0) & (key_offset <= 2 * window_half)

    def one_block(block_index):
        row_start = (block_index * block_rows).astype(jnp.int32)
        query_block = lax.dynamic_slice_in_dim(query_rows, row_start, block_rows, 0).astype(jnp.float32)
        query_block = query_block.reshape(block_rows, HEADS_W, HD)
        kv_block = lax.dynamic_slice_in_dim(padded_kv, row_start, key_span, 0).astype(jnp.float32)
        key_part = kv_block[:, :HW].reshape(key_span, HEADS_W, HD)
        value_part = kv_block[:, HW:].reshape(key_span, HEADS_W, HD)
        query_seg = lax.dynamic_slice_in_dim(segments, row_start, block_rows, 0)
        key_seg = lax.dynamic_slice_in_dim(padded_seg, row_start, key_span, 0)
        allowed = in_window & (query_seg[:, None] == key_seg[None, :])
        scores = jnp.einsum('qhe,khe->hqk', query_block, key_part) / math.sqrt(HD)
        scores = jnp.where(allowed[None], scores, masked_score)
        row_max = lax.optimization_barrier(jnp.max(scores, axis=2, keepdims=True))
        exp_scores = jnp.exp(scores - row_max)
        attn_probs = (exp_scores / lax.optimization_barrier(jnp.sum(exp_scores, axis=2, keepdims=True))).astype(jnp.bfloat16)
        context = jnp.einsum('hqk,khe->qhe', attn_probs.astype(jnp.float32), value_part)
        return context.reshape(block_rows, HW).astype(jnp.bfloat16)
    blocks = lax.map(one_block, jnp.arange(block_count, dtype=jnp.int32))
    return blocks.reshape(FRAMES, HW)

def conv_sequence(residual, cotangent_rows, segments, kernel_float):
    conv_lead = KW // 2
    padded_res = jnp.pad(residual.astype(jnp.float32), ((conv_lead, conv_lead), (0, 0)))
    padded_seg = jnp.pad(segments, (conv_lead, conv_lead), constant_values=-1)
    conv_out = jnp.zeros((FRAMES, D), jnp.float32)
    for offset in range(KW):
        same_utt = (padded_seg[offset:offset + FRAMES] == segments)[:, None]
        conv_out = conv_out + jnp.where(same_utt, kernel_float[offset] * padded_res[offset:offset + FRAMES], 0.0)
    gate_sig = jax.nn.sigmoid(conv_out)
    gated_grad = cotangent_rows.astype(jnp.float32) * gate_sig * (1.0 + conv_out * (1.0 - gate_sig))
    padded_grad = jnp.pad(gated_grad, ((conv_lead, conv_lead), (0, 0)))
    back_sum = cotangent_rows.astype(jnp.float32)
    kernel_rows = []
    for offset in range(KW):
        lower = KW - offset
        same_back = (padded_seg[lower:lower + FRAMES] == segments)[:, None]
        back_sum = back_sum + jnp.where(same_back, kernel_float[offset] * padded_grad[lower:lower + FRAMES], 0.0)
        same_utt = (padded_seg[offset:offset + FRAMES] == segments)[:, None]
        kernel_rows.append(lax.optimization_barrier(jnp.sum(jnp.where(same_utt, gated_grad * padded_res[offset:offset + FRAMES], 0.0), axis=0)))
    return (back_sum.astype(jnp.bfloat16), jnp.stack(kernel_rows))

def reference(queries, keys_values, inputs, cotangent, out_weight, conv_kernel, utt_starts):
    kernel_float = conv_kernel.astype(jnp.float32)

    def one_sequence(sequence_item):
        query_rows, kv_rows, input_rows, cotangent_rows, starts_row = sequence_item
        segments = segment_ids(starts_row, jnp.arange(FRAMES, dtype=jnp.int32))
        context = attend_sequence(query_rows, kv_rows, segments)
        residual = (input_rows.astype(jnp.float32) + jnp.dot(context, out_weight, preferred_element_type=jnp.float32)).astype(jnp.bfloat16)
        residual_grad, kernel_rows = conv_sequence(residual, cotangent_rows, segments, kernel_float)
        context_grad = lax.dot_general(residual_grad, out_weight, (((1,), (1,)), ((), ())), preferred_element_type=jnp.float32).astype(jnp.bfloat16)
        weight_rows = lax.dot_general(context, residual_grad, (((0,), (0,)), ((), ())), preferred_element_type=jnp.float32)
        return (context_grad, weight_rows, kernel_rows)
    context_grad, weight_parts, kernel_parts = lax.map(one_sequence, (queries, keys_values, inputs, cotangent, utt_starts))
    grad_scale = 1.0 / math.sqrt(SEQS * FRAMES)
    return (context_grad, lax.optimization_barrier(jnp.sum(weight_parts, axis=0)) * grad_scale, lax.optimization_barrier(jnp.sum(kernel_parts, axis=0)) * grad_scale)
```

```python
import math

import jax
import jax.numpy as jnp
from jax import lax
from jax.sharding import Mesh, PartitionSpec as P

HEADS_W = 8
KW = 32
WIN = 128


masked_score = -1e30

TM_AXES = ("z", "y_hi", "core")
FSDP_AXES = ("x", "y_lo")
TM = TM_AXES
FSDP = FSDP_AXES


def halve_over_fsdp(parts):
    size = parts.shape[0]
    own = lax.axis_index(FSDP)
    bits = [1 << k for k in range(size.bit_length() - 1)]
    acc = parts.reshape((2,) * len(bits) + parts.shape[1:])
    for depth, bit in enumerate(bits):
        axis = len(bits) - 1 - depth
        mine = (own & bit) != 0
        low = lax.index_in_dim(acc, 0, axis, keepdims=False)
        high = lax.index_in_dim(acc, 1, axis, keepdims=False)
        keep = jnp.where(mine, high, low)
        send = jnp.where(mine, low, high).astype(jnp.bfloat16)
        pairs = [(i, i ^ bit) for i in range(size)]
        acc = keep + lax.ppermute(send, FSDP, pairs).astype(jnp.float32)
    return acc


def reduce_over_tm(share):
    sizes = [(axis, lax.axis_size(axis)) for axis in reversed(TM_AXES)]
    acc = share
    for axis, n in sizes:
        acc = lax.all_to_all(acc.reshape(n, -1), axis, 0, 0, tiled=True).sum(axis=0)
    for axis, n in reversed(sizes):
        spread = jnp.broadcast_to(acc[None], (n,) + acc.shape)
        acc = lax.all_to_all(spread, axis, 0, 0, tiled=True).reshape(-1)
    return acc


def with_halo(x, sides, width):
    for axis, dim in sides:
        devices, length = (lax.axis_size(axis), x.shape[dim])
        up = [(i, (i + 1) % devices) for i in range(devices - 1)]
        down = [(j, i) for i, j in up]
        last = lax.slice_in_dim(x, length - width, length, axis=dim)
        initial = lax.slice_in_dim(x, 0, width, axis=dim)
        before = lax.ppermute(last, axis, up)
        after = lax.ppermute(initial, axis, down)
        x = jnp.concatenate([before, x, after], axis=dim)
    return x


def segment_ids(starts_row, positions):
    return jnp.sum((starts_row[None, :] <= positions[:, None]).astype(jnp.int32), axis=1) - 1


def shards(queries, keys_values, inputs, cotangent, out_weight, conv_kernel, utt_starts):
    query_rows = queries[0]
    kv_rows = keys_values[0]
    input_rows = inputs[0]
    cotangent_rows = cotangent[0]
    starts_row = utt_starts[0]
    local_frames = query_rows.shape[0]
    head_width = query_rows.shape[1]
    head_size = head_width // HEADS_W
    window_half = WIN // 2
    conv_reach = KW - 1
    conv_lead = KW // 2
    conv_span = local_frames + KW - 1
    frames_total = local_frames * lax.axis_size(TM)
    first_frame = lax.axis_index(TM) * local_frames
    full_weight, full_kernel = (
        lax.all_gather(out_weight, FSDP, axis=0, tiled=True),
        lax.all_gather(conv_kernel, FSDP, axis=1, tiled=True),
    )
    kv_ext = with_halo(kv_rows, ((TM, 0),), window_half)
    key_span = local_frames + 2 * window_half
    key_positions = first_frame - window_half + jnp.arange(key_span, dtype=jnp.int32)
    key_seg = jnp.where(key_positions < frames_total, segment_ids(starts_row, key_positions), -1)
    query_seg = segment_ids(starts_row, first_frame + jnp.arange(local_frames, dtype=jnp.int32))
    key_offset = (
        jnp.arange(key_span, dtype=jnp.int32)[None, :]
        - jnp.arange(local_frames, dtype=jnp.int32)[:, None]
    )
    allowed = (
        (key_offset >= 0)
        & (key_offset <= 2 * window_half)
        & (query_seg[:, None] == key_seg[None, :])
    )
    query_heads = query_rows.reshape(local_frames, HEADS_W, head_size)
    key_heads = kv_ext[:, :head_width].reshape(key_span, HEADS_W, head_size)
    value_heads = kv_ext[:, head_width:].reshape(key_span, HEADS_W, head_size)
    scores = jnp.einsum(
        "qhe,khe->hqk", query_heads, key_heads, preferred_element_type=jnp.float32
    ) / math.sqrt(head_size)
    scores = jnp.where(allowed[None], scores, masked_score)
    row_max = jnp.max(scores, axis=2, keepdims=True)
    exp_scores = jnp.exp(scores - row_max)
    attn_probs = (exp_scores / jnp.sum(exp_scores, axis=2, keepdims=True)).astype(jnp.bfloat16)
    context = jnp.einsum(
        "hqk,khe->qhe", attn_probs, value_heads, preferred_element_type=jnp.float32
    )
    context = context.reshape(local_frames, head_width).astype(jnp.bfloat16)
    residual = (
        input_rows.astype(jnp.float32)
        + jnp.dot(context, full_weight, preferred_element_type=jnp.float32)
    ).astype(jnp.bfloat16)
    stacked_rims = with_halo(jnp.stack([residual, cotangent_rows]), ((TM, 1),), conv_reach)
    residual_ext = stacked_rims[0]
    cotangent_ext = stacked_rims[1][conv_lead : conv_lead + conv_span]
    residual_positions = (
        first_frame - conv_reach + jnp.arange(local_frames + 2 * conv_reach, dtype=jnp.int32)
    )
    residual_seg = segment_ids(starts_row, residual_positions)
    conv_seg = residual_seg[conv_lead : conv_lead + conv_span]
    own_seg = residual_seg[conv_reach : conv_reach + local_frames]
    kernel_float = full_kernel.astype(jnp.float32)
    conv_out = jnp.zeros((conv_span, residual.shape[1]), jnp.float32)
    for offset in range(KW):
        same_utt = (conv_seg == residual_seg[offset : offset + conv_span])[:, None]
        conv_out = conv_out + jnp.where(
            same_utt,
            kernel_float[offset] * residual_ext[offset : offset + conv_span].astype(jnp.float32),
            0.0,
        )
    gate_sig = jax.nn.sigmoid(conv_out)
    gated_grad = cotangent_ext.astype(jnp.float32) * gate_sig * (1.0 + conv_out * (1.0 - gate_sig))
    back_sum = cotangent_rows.astype(jnp.float32)
    own_lower = conv_lead - 1
    own_grad = gated_grad[own_lower : own_lower + local_frames]
    own_conv_seg = conv_seg[own_lower : own_lower + local_frames]
    for offset in range(KW):
        lower = KW - 1 - offset
        same_back = (conv_seg[lower : lower + local_frames] == own_seg)[:, None]
        back_sum = back_sum + jnp.where(
            same_back, kernel_float[offset] * gated_grad[lower : lower + local_frames], 0.0
        )
    products = jnp.stack(
        [
            jnp.where(
                (
                    own_conv_seg
                    == residual_seg[own_lower + offset : own_lower + offset + local_frames]
                )[:, None],
                own_grad
                * residual_ext[own_lower + offset : own_lower + offset + local_frames].astype(
                    jnp.float32
                ),
                0.0,
            )
            for offset in range(KW)
        ]
    )
    kernel_part = jnp.sum(products, axis=1)
    residual_grad = back_sum.astype(jnp.bfloat16)
    context_grad = lax.dot_general(
        residual_grad, full_weight, (((1,), (1,)), ((), ())), preferred_element_type=jnp.float32
    ).astype(jnp.bfloat16)
    grad_scale = 1.0 / math.sqrt(lax.axis_size(FSDP) * queries.shape[0] * frames_total)
    weight_part = lax.dot_general(
        context, residual_grad, (((0,), (0,)), ((), ())), preferred_element_type=jnp.float32
    )
    fsdp_size = lax.axis_size(FSDP)
    kernel_rows = kernel_part.reshape(KW, fsdp_size, -1).transpose(1, 0, 2)
    grad_parts = jnp.concatenate(
        [weight_part.reshape(fsdp_size, -1), kernel_rows.reshape(fsdp_size, -1)], axis=1
    ) * grad_scale
    grad_share = reduce_over_tm(halve_over_fsdp(grad_parts))
    weight_size = weight_part.size // fsdp_size
    weight_grad = grad_share[:weight_size].reshape(-1, weight_part.shape[1])
    kernel_grad = grad_share[weight_size:].reshape(KW, -1)
    return (context_grad[None], weight_grad, kernel_grad)


def solution(mesh):
    tm_size, fsdp_size = mesh.shape["tm"], mesh.shape["fsdp"]
    sub_mesh = Mesh(
        mesh.devices.reshape(tm_size // 8, 4, 2, fsdp_size // 2, 2), TM_AXES + FSDP_AXES
    )
    return jax.shard_map(
        shards,
        mesh=sub_mesh,
        in_specs=(
            P(FSDP, TM, None),
            P(FSDP, TM, None),
            P(FSDP, TM, None),
            P(FSDP, TM, None),
            P(FSDP, None),
            P(None, FSDP),
            P(FSDP, None),
        ),
        out_specs=(P(FSDP, TM, None), P(FSDP, None), P(None, FSDP)),
        check_vma=False,
    )
```

```python
import math

import jax
import jax.numpy as jnp
from jax import lax
from jax.sharding import Mesh, PartitionSpec as P

HEADS_W = 8
KW = 32
WIN = 128


masked_score = -1e30

TM_AXES = ("z", "y_hi", "core")
FSDP_AXES = ("x", "y_lo")
TM = TM_AXES
FSDP = FSDP_AXES


def halve_over_fsdp(parts):
    size = parts.shape[0]
    own = lax.axis_index(FSDP)
    bits = [1 << k for k in range(size.bit_length() - 1)]
    acc = parts.reshape((2,) * len(bits) + parts.shape[1:])
    for depth, bit in enumerate(bits):
        axis = len(bits) - 1 - depth
        mine = (own & bit) != 0
        low = lax.index_in_dim(acc, 0, axis, keepdims=False)
        high = lax.index_in_dim(acc, 1, axis, keepdims=False)
        keep = jnp.where(mine, high, low)
        send = jnp.where(mine, low, high).astype(jnp.bfloat16)
        pairs = [(i, i ^ bit) for i in range(size)]
        acc = keep + lax.ppermute(send, FSDP, pairs).astype(jnp.float32)
    return acc


def reduce_over_tm(share):
    sizes = [(axis, lax.axis_size(axis)) for axis in reversed(TM_AXES)]
    acc = share
    for axis, n in sizes:
        pieces = acc.reshape(n, -1).astype(jnp.bfloat16)
        acc = lax.all_to_all(pieces, axis, 0, 0, tiled=True).astype(jnp.float32).sum(axis=0)
    for axis, n in reversed(sizes):
        spread = jnp.broadcast_to(acc[None], (n,) + acc.shape)
        acc = lax.all_to_all(spread, axis, 0, 0, tiled=True).reshape(-1)
    return acc


def with_halo(x, sides, width):
    for axis, dim in sides:
        devices, length = (lax.axis_size(axis), x.shape[dim])
        up = [(i, (i + 1) % devices) for i in range(devices - 1)]
        down = [(j, i) for i, j in up]
        last = lax.slice_in_dim(x, length - width, length, axis=dim)
        initial = lax.slice_in_dim(x, 0, width, axis=dim)
        before = lax.ppermute(last, axis, up)
        after = lax.ppermute(initial, axis, down)
        x = jnp.concatenate([before, x, after], axis=dim)
    return x


def segment_ids(starts_row, positions):
    return jnp.sum((starts_row[None, :] <= positions[:, None]).astype(jnp.int32), axis=1) - 1


def shards(queries, keys_values, inputs, cotangent, out_weight, conv_kernel, utt_starts):
    query_rows = queries[0]
    kv_rows = keys_values[0]
    input_rows = inputs[0]
    cotangent_rows = cotangent[0]
    starts_row = utt_starts[0]
    local_frames = query_rows.shape[0]
    head_width = query_rows.shape[1]
    head_size = head_width // HEADS_W
    window_half = WIN // 2
    conv_reach = KW - 1
    conv_lead = KW // 2
    conv_span = local_frames + KW - 1
    frames_total = local_frames * lax.axis_size(TM)
    first_frame = lax.axis_index(TM) * local_frames
    weight_rows, kernel_cols = out_weight.shape[0], conv_kernel.shape[1]
    gathered = lax.all_gather(
        jnp.concatenate([out_weight, conv_kernel.reshape(-1, out_weight.shape[1])]), FSDP
    )
    full_weight = gathered[:, :weight_rows].reshape(-1, out_weight.shape[1])
    full_kernel = (
        gathered[:, weight_rows:].reshape(-1, KW, kernel_cols).transpose(1, 0, 2).reshape(KW, -1)
    )
    kv_ext = with_halo(kv_rows, ((TM, 0),), window_half)
    key_span = local_frames + 2 * window_half
    key_positions = first_frame - window_half + jnp.arange(key_span, dtype=jnp.int32)
    key_seg = jnp.where(key_positions < frames_total, segment_ids(starts_row, key_positions), -1)
    query_seg = segment_ids(starts_row, first_frame + jnp.arange(local_frames, dtype=jnp.int32))
    key_offset = (
        jnp.arange(key_span, dtype=jnp.int32)[None, :]
        - jnp.arange(local_frames, dtype=jnp.int32)[:, None]
    )
    allowed = (
        (key_offset >= 0)
        & (key_offset <= 2 * window_half)
        & (query_seg[:, None] == key_seg[None, :])
    )
    query_heads = query_rows.reshape(local_frames, HEADS_W, head_size)
    key_heads = kv_ext[:, :head_width].reshape(key_span, HEADS_W, head_size)
    value_heads = kv_ext[:, head_width:].reshape(key_span, HEADS_W, head_size)
    scores = jnp.einsum(
        "qhe,khe->hqk", query_heads, key_heads, preferred_element_type=jnp.float32
    ) / math.sqrt(head_size)
    scores = jnp.where(allowed[None], scores, masked_score)
    row_max = jnp.max(scores, axis=2, keepdims=True)
    exp_scores = jnp.exp(scores - row_max)
    attn_probs = (exp_scores / jnp.sum(exp_scores, axis=2, keepdims=True)).astype(jnp.bfloat16)
    context = jnp.einsum(
        "hqk,khe->qhe", attn_probs, value_heads, preferred_element_type=jnp.float32
    )
    context = context.reshape(local_frames, head_width).astype(jnp.bfloat16)
    residual = (
        input_rows.astype(jnp.float32)
        + jnp.dot(context, full_weight, preferred_element_type=jnp.float32)
    ).astype(jnp.bfloat16)
    stacked_rims = with_halo(jnp.stack([residual, cotangent_rows]), ((TM, 1),), conv_reach)
    residual_ext = stacked_rims[0]
    cotangent_ext = stacked_rims[1][conv_lead : conv_lead + conv_span]
    residual_positions = (
        first_frame - conv_reach + jnp.arange(local_frames + 2 * conv_reach, dtype=jnp.int32)
    )
    residual_seg = segment_ids(starts_row, residual_positions)
    conv_seg = residual_seg[conv_lead : conv_lead + conv_span]
    own_seg = residual_seg[conv_reach : conv_reach + local_frames]
    kernel_float = full_kernel.astype(jnp.float32)
    conv_out = jnp.zeros((conv_span, residual.shape[1]), jnp.float32)
    for offset in range(KW):
        same_utt = (conv_seg == residual_seg[offset : offset + conv_span])[:, None]
        conv_out = conv_out + jnp.where(
            same_utt,
            kernel_float[offset] * residual_ext[offset : offset + conv_span].astype(jnp.float32),
            0.0,
        )
    gate_sig = jax.nn.sigmoid(conv_out)
    gated_grad = cotangent_ext.astype(jnp.float32) * gate_sig * (1.0 + conv_out * (1.0 - gate_sig))
    back_sum = cotangent_rows.astype(jnp.float32)
    own_lower = conv_lead - 1
    own_grad = gated_grad[own_lower : own_lower + local_frames]
    own_conv_seg = conv_seg[own_lower : own_lower + local_frames]
    for offset in range(KW):
        lower = KW - 1 - offset
        same_back = (conv_seg[lower : lower + local_frames] == own_seg)[:, None]
        back_sum = back_sum + jnp.where(
            same_back, kernel_float[offset] * gated_grad[lower : lower + local_frames], 0.0
        )
    products = jnp.stack(
        [
            jnp.where(
                (
                    own_conv_seg
                    == residual_seg[own_lower + offset : own_lower + offset + local_frames]
                )[:, None],
                own_grad
                * residual_ext[own_lower + offset : own_lower + offset + local_frames].astype(
                    jnp.float32
                ),
                0.0,
            )
            for offset in range(KW)
        ]
    )
    kernel_part = jnp.sum(products, axis=1)
    residual_grad = back_sum.astype(jnp.bfloat16)
    context_grad = lax.dot_general(
        residual_grad, full_weight, (((1,), (1,)), ((), ())), preferred_element_type=jnp.float32
    ).astype(jnp.bfloat16)
    grad_scale = 1.0 / math.sqrt(lax.axis_size(FSDP) * queries.shape[0] * frames_total)
    weight_part = lax.dot_general(
        context, residual_grad, (((0,), (0,)), ((), ())), preferred_element_type=jnp.float32
    )
    fsdp_size = lax.axis_size(FSDP)
    kernel_rows = kernel_part.reshape(KW, fsdp_size, -1).transpose(1, 0, 2)
    grad_parts = jnp.concatenate(
        [weight_part.reshape(fsdp_size, -1), kernel_rows.reshape(fsdp_size, -1)], axis=1
    ) * grad_scale
    grad_share = reduce_over_tm(halve_over_fsdp(grad_parts))
    weight_size = weight_part.size // fsdp_size
    weight_grad = grad_share[:weight_size].reshape(-1, weight_part.shape[1])
    kernel_grad = grad_share[weight_size:].reshape(KW, -1)
    return (context_grad[None], weight_grad, kernel_grad)


def solution(mesh):
    tm_size, fsdp_size = mesh.shape["tm"], mesh.shape["fsdp"]
    sub_mesh = Mesh(
        mesh.devices.reshape(tm_size // 8, 4, 2, fsdp_size // 2, 2), TM_AXES + FSDP_AXES
    )
    return jax.shard_map(
        shards,
        mesh=sub_mesh,
        in_specs=(
            P(FSDP, TM, None),
            P(FSDP, TM, None),
            P(FSDP, TM, None),
            P(FSDP, TM, None),
            P(FSDP, None),
            P(None, FSDP),
            P(FSDP, None),
        ),
        out_specs=(P(FSDP, TM, None), P(FSDP, None), P(None, FSDP)),
        check_vma=False,
    )
```

```python
import math

import jax
import jax.numpy as jnp
from jax import lax
from jax.sharding import Mesh, PartitionSpec as P

HEADS_W = 8
KW = 32
WIN = 128


masked_score = -1e30

TM_AXES = ("z", "y_hi", "core")
FSDP_AXES = ("x", "y_lo")
TM = TM_AXES
FSDP = FSDP_AXES
CORE = "core"


def halve_over_fsdp(parts):
    size = parts.shape[0]
    own = lax.axis_index(FSDP)
    bits = [1 << k for k in range(size.bit_length() - 1)]
    acc = parts.reshape((2,) * len(bits) + parts.shape[1:])
    for depth, bit in enumerate(bits):
        axis = len(bits) - 1 - depth
        mine = (own & bit) != 0
        low = lax.index_in_dim(acc, 0, axis, keepdims=False)
        high = lax.index_in_dim(acc, 1, axis, keepdims=False)
        keep = jnp.where(mine, high, low)
        send = jnp.where(mine, low, high).astype(jnp.bfloat16)
        pairs = [(i, i ^ bit) for i in range(size)]
        acc = keep + lax.ppermute(send, FSDP, pairs).astype(jnp.float32)
    return acc


def split_over_core(x, axis):
    half = x.shape[axis] // 2
    mine = lax.axis_index(CORE) != 0
    return jnp.where(
        mine, lax.slice_in_dim(x, half, 2 * half, axis=axis), lax.slice_in_dim(x, 0, half, axis=axis)
    )


def join_over_core(x, axis):
    other = lax.ppermute(x, CORE, [(0, 1), (1, 0)])
    mine = lax.axis_index(CORE) != 0
    return jnp.where(
        mine, jnp.concatenate([other, x], axis=axis), jnp.concatenate([x, other], axis=axis)
    )


def halve_over_core(parts):
    half = parts.shape[-1] // 2
    mine = lax.axis_index(CORE) != 0
    low, high = parts[..., :half], parts[..., half:]
    keep = jnp.where(mine, high, low)
    send = jnp.where(mine, low, high)
    return keep + lax.ppermute(send, CORE, [(0, 1), (1, 0)])


def reduce_over_tm(share):
    sizes = [(axis, lax.axis_size(axis)) for axis in reversed(TM_AXES) if axis != CORE]
    acc = share
    for axis, n in sizes:
        pieces = acc.reshape(n, -1).astype(jnp.bfloat16)
        acc = lax.all_to_all(pieces, axis, 0, 0, tiled=True).astype(jnp.float32).sum(axis=0)
    for axis, n in reversed(sizes):
        spread = jnp.broadcast_to(acc[None], (n,) + acc.shape)
        acc = lax.all_to_all(spread, axis, 0, 0, tiled=True).reshape(-1)
    return acc


def with_halo(x, sides, width):
    for axis, dim in sides:
        devices, length = (lax.axis_size(axis), x.shape[dim])
        up = [(i, (i + 1) % devices) for i in range(devices - 1)]
        down = [(j, i) for i, j in up]
        last = lax.slice_in_dim(x, length - width, length, axis=dim)
        initial = lax.slice_in_dim(x, 0, width, axis=dim)
        before = lax.ppermute(last, axis, up)
        after = lax.ppermute(initial, axis, down)
        x = jnp.concatenate([before, x, after], axis=dim)
    return x


def segment_ids(starts_row, positions):
    return jnp.sum((starts_row[None, :] <= positions[:, None]).astype(jnp.int32), axis=1) - 1


def shards(queries, keys_values, inputs, cotangent, out_weight, conv_kernel, utt_starts):
    query_rows = queries[0]
    kv_rows = keys_values[0]
    input_rows = inputs[0]
    cotangent_rows = cotangent[0]
    starts_row = utt_starts[0]
    local_frames = query_rows.shape[0]
    head_width = query_rows.shape[1]
    head_size = head_width // HEADS_W
    window_half = WIN // 2
    conv_reach = KW - 1
    conv_lead = KW // 2
    conv_span = local_frames + KW - 1
    frames_total = local_frames * lax.axis_size(TM)
    first_frame = lax.axis_index(TM) * local_frames
    weight_rows, kernel_cols = out_weight.shape[0], conv_kernel.shape[1]
    gathered = join_over_core(
        lax.all_gather(
            split_over_core(
                jnp.concatenate([out_weight, conv_kernel.reshape(-1, out_weight.shape[1])]), 1
            ),
            FSDP,
        ),
        2,
    )
    full_weight = gathered[:, :weight_rows].reshape(-1, out_weight.shape[1])
    full_kernel = (
        gathered[:, weight_rows:].reshape(-1, KW, kernel_cols).transpose(1, 0, 2).reshape(KW, -1)
    )
    kv_ext = with_halo(kv_rows, ((TM, 0),), window_half)
    key_span = local_frames + 2 * window_half
    key_positions = first_frame - window_half + jnp.arange(key_span, dtype=jnp.int32)
    key_seg = jnp.where(key_positions < frames_total, segment_ids(starts_row, key_positions), -1)
    query_seg = segment_ids(starts_row, first_frame + jnp.arange(local_frames, dtype=jnp.int32))
    key_offset = (
        jnp.arange(key_span, dtype=jnp.int32)[None, :]
        - jnp.arange(local_frames, dtype=jnp.int32)[:, None]
    )
    allowed = (
        (key_offset >= 0)
        & (key_offset <= 2 * window_half)
        & (query_seg[:, None] == key_seg[None, :])
    )
    query_heads = query_rows.reshape(local_frames, HEADS_W, head_size)
    key_heads = kv_ext[:, :head_width].reshape(key_span, HEADS_W, head_size)
    value_heads = kv_ext[:, head_width:].reshape(key_span, HEADS_W, head_size)
    scores = jnp.einsum(
        "qhe,khe->hqk", query_heads, key_heads, preferred_element_type=jnp.float32
    ) / math.sqrt(head_size)
    scores = jnp.where(allowed[None], scores, masked_score)
    row_max = jnp.max(scores, axis=2, keepdims=True)
    exp_scores = jnp.exp(scores - row_max)
    attn_probs = (exp_scores / jnp.sum(exp_scores, axis=2, keepdims=True)).astype(jnp.bfloat16)
    context = jnp.einsum(
        "hqk,khe->qhe", attn_probs, value_heads, preferred_element_type=jnp.float32
    )
    context = context.reshape(local_frames, head_width).astype(jnp.bfloat16)
    residual = (
        input_rows.astype(jnp.float32)
        + jnp.dot(context, full_weight, preferred_element_type=jnp.float32)
    ).astype(jnp.bfloat16)
    stacked_rims = with_halo(jnp.stack([residual, cotangent_rows]), ((TM, 1),), conv_reach)
    residual_ext = stacked_rims[0]
    cotangent_ext = stacked_rims[1][conv_lead : conv_lead + conv_span]
    residual_positions = (
        first_frame - conv_reach + jnp.arange(local_frames + 2 * conv_reach, dtype=jnp.int32)
    )
    residual_seg = segment_ids(starts_row, residual_positions)
    conv_seg = residual_seg[conv_lead : conv_lead + conv_span]
    own_seg = residual_seg[conv_reach : conv_reach + local_frames]
    kernel_float = full_kernel.astype(jnp.float32)
    conv_out = jnp.zeros((conv_span, residual.shape[1]), jnp.float32)
    for offset in range(KW):
        same_utt = (conv_seg == residual_seg[offset : offset + conv_span])[:, None]
        conv_out = conv_out + jnp.where(
            same_utt,
            kernel_float[offset] * residual_ext[offset : offset + conv_span].astype(jnp.float32),
            0.0,
        )
    gate_sig = jax.nn.sigmoid(conv_out)
    gated_grad = cotangent_ext.astype(jnp.float32) * gate_sig * (1.0 + conv_out * (1.0 - gate_sig))
    back_sum = cotangent_rows.astype(jnp.float32)
    own_lower = conv_lead - 1
    own_grad = gated_grad[own_lower : own_lower + local_frames]
    own_conv_seg = conv_seg[own_lower : own_lower + local_frames]
    for offset in range(KW):
        lower = KW - 1 - offset
        same_back = (conv_seg[lower : lower + local_frames] == own_seg)[:, None]
        back_sum = back_sum + jnp.where(
            same_back, kernel_float[offset] * gated_grad[lower : lower + local_frames], 0.0
        )
    products = jnp.stack(
        [
            jnp.where(
                (
                    own_conv_seg
                    == residual_seg[own_lower + offset : own_lower + offset + local_frames]
                )[:, None],
                own_grad
                * residual_ext[own_lower + offset : own_lower + offset + local_frames].astype(
                    jnp.float32
                ),
                0.0,
            )
            for offset in range(KW)
        ]
    )
    kernel_part = jnp.sum(products, axis=1)
    residual_grad = back_sum.astype(jnp.bfloat16)
    context_grad = lax.dot_general(
        residual_grad, full_weight, (((1,), (1,)), ((), ())), preferred_element_type=jnp.float32
    ).astype(jnp.bfloat16)
    grad_scale = 1.0 / math.sqrt(lax.axis_size(FSDP) * queries.shape[0] * frames_total)
    weight_part = lax.dot_general(
        context, residual_grad, (((0,), (0,)), ((), ())), preferred_element_type=jnp.float32
    )
    fsdp_size = lax.axis_size(FSDP)
    kernel_rows = kernel_part.reshape(KW, fsdp_size, -1).transpose(1, 0, 2)
    grad_parts = jnp.concatenate(
        [weight_part.reshape(fsdp_size, -1), kernel_rows.reshape(fsdp_size, -1)], axis=1
    ) * grad_scale
    grad_share = join_over_core(reduce_over_tm(halve_over_fsdp(halve_over_core(grad_parts))), 0)
    weight_size = weight_part.size // fsdp_size
    weight_grad = grad_share[:weight_size].reshape(-1, weight_part.shape[1])
    kernel_grad = grad_share[weight_size:].reshape(KW, -1)
    return (context_grad[None], weight_grad, kernel_grad)


def solution(mesh):
    tm_size, fsdp_size = mesh.shape["tm"], mesh.shape["fsdp"]
    sub_mesh = Mesh(
        mesh.devices.reshape(tm_size // 8, 4, 2, fsdp_size // 2, 2), TM_AXES + FSDP_AXES
    )
    return jax.shard_map(
        shards,
        mesh=sub_mesh,
        in_specs=(
            P(FSDP, TM, None),
            P(FSDP, TM, None),
            P(FSDP, TM, None),
            P(FSDP, TM, None),
            P(FSDP, None),
            P(None, FSDP),
            P(FSDP, None),
        ),
        out_specs=(P(FSDP, TM, None), P(FSDP, None), P(None, FSDP)),
        check_vma=False,
    )
```

```python
import math

import jax
import jax.numpy as jnp
from jax import lax
from jax.sharding import Mesh, PartitionSpec as P

HEADS_W = 8
KW = 32
WIN = 128


masked_score = -1e30

TM_AXES = ("z", "y_hi", "core")
FSDP_AXES = ("x", "y_lo")
TM = TM_AXES
FSDP = FSDP_AXES
CORE = "core"


def halve_over_fsdp(parts):
    size = parts.shape[0]
    own = lax.axis_index(FSDP)
    bits = [1 << k for k in range(size.bit_length() - 1)]
    acc = parts.reshape((2,) * len(bits) + parts.shape[1:])
    for depth, bit in enumerate(bits):
        axis = len(bits) - 1 - depth
        mine = (own & bit) != 0
        low = lax.index_in_dim(acc, 0, axis, keepdims=False)
        high = lax.index_in_dim(acc, 1, axis, keepdims=False)
        keep = jnp.where(mine, high, low)
        send = jnp.where(mine, low, high).astype(jnp.bfloat16)
        pairs = [(i, i ^ bit) for i in range(size)]
        acc = keep + lax.ppermute(send, FSDP, pairs).astype(jnp.float32)
    return acc


def double_over_fsdp(shard):
    size = lax.axis_size(FSDP)
    own = lax.axis_index(FSDP)
    bits = [1 << k for k in range(size.bit_length() - 1)]
    acc = shard
    for bit in reversed(bits):
        pairs = [(i, i ^ bit) for i in range(size)]
        got = lax.ppermute(acc, FSDP, pairs)
        acc = jnp.where((own & bit) != 0, jnp.stack([got, acc]), jnp.stack([acc, got]))
    order = tuple(reversed(range(len(bits)))) + tuple(range(len(bits), acc.ndim))
    return acc.transpose(order).reshape((size,) + shard.shape)


def split_over_core(x, axis):
    half = x.shape[axis] // 2
    mine = lax.axis_index(CORE) != 0
    return jnp.where(
        mine, lax.slice_in_dim(x, half, 2 * half, axis=axis), lax.slice_in_dim(x, 0, half, axis=axis)
    )


def join_over_core(x, axis):
    other = lax.ppermute(x, CORE, [(0, 1), (1, 0)])
    mine = lax.axis_index(CORE) != 0
    return jnp.where(
        mine, jnp.concatenate([other, x], axis=axis), jnp.concatenate([x, other], axis=axis)
    )


def halve_over_core(parts):
    half = parts.shape[-1] // 2
    mine = lax.axis_index(CORE) != 0
    low, high = parts[..., :half], parts[..., half:]
    keep = jnp.where(mine, high, low)
    send = jnp.where(mine, low, high)
    return keep + lax.ppermute(send, CORE, [(0, 1), (1, 0)])


def reduce_over_tm(share):
    sizes = [(axis, lax.axis_size(axis)) for axis in reversed(TM_AXES) if axis != CORE]
    acc = share
    for axis, n in sizes:
        pieces = acc.reshape(n, -1).astype(jnp.bfloat16)
        acc = lax.all_to_all(pieces, axis, 0, 0, tiled=True).astype(jnp.float32).sum(axis=0)
    for axis, n in reversed(sizes):
        spread = jnp.broadcast_to(acc[None], (n,) + acc.shape)
        acc = lax.all_to_all(spread, axis, 0, 0, tiled=True).reshape(-1)
    return acc


def with_halo(x, sides, width):
    for axis, dim in sides:
        devices, length = (lax.axis_size(axis), x.shape[dim])
        up = [(i, (i + 1) % devices) for i in range(devices - 1)]
        down = [(j, i) for i, j in up]
        last = lax.slice_in_dim(x, length - width, length, axis=dim)
        initial = lax.slice_in_dim(x, 0, width, axis=dim)
        before = lax.ppermute(last, axis, up)
        after = lax.ppermute(initial, axis, down)
        x = jnp.concatenate([before, x, after], axis=dim)
    return x


def segment_ids(starts_row, positions):
    return jnp.sum((starts_row[None, :] <= positions[:, None]).astype(jnp.int32), axis=1) - 1


def shards(queries, keys_values, inputs, cotangent, out_weight, conv_kernel, utt_starts):
    query_rows = queries[0]
    kv_rows = keys_values[0]
    input_rows = inputs[0]
    cotangent_rows = cotangent[0]
    starts_row = utt_starts[0]
    local_frames = query_rows.shape[0]
    head_width = query_rows.shape[1]
    head_size = head_width // HEADS_W
    window_half = WIN // 2
    conv_reach = KW - 1
    conv_lead = KW // 2
    conv_span = local_frames + KW - 1
    frames_total = local_frames * lax.axis_size(TM)
    first_frame = lax.axis_index(TM) * local_frames
    weight_rows, kernel_cols = out_weight.shape[0], conv_kernel.shape[1]
    gathered = join_over_core(
        double_over_fsdp(
            split_over_core(
                jnp.concatenate([out_weight, conv_kernel.reshape(-1, out_weight.shape[1])]), 1
            )
        ),
        2,
    )
    full_weight = gathered[:, :weight_rows].reshape(-1, out_weight.shape[1])
    full_kernel = (
        gathered[:, weight_rows:].reshape(-1, KW, kernel_cols).transpose(1, 0, 2).reshape(KW, -1)
    )
    kv_ext = with_halo(kv_rows, ((TM, 0),), window_half)
    key_span = local_frames + 2 * window_half
    key_positions = first_frame - window_half + jnp.arange(key_span, dtype=jnp.int32)
    key_seg = jnp.where(key_positions < frames_total, segment_ids(starts_row, key_positions), -1)
    query_seg = segment_ids(starts_row, first_frame + jnp.arange(local_frames, dtype=jnp.int32))
    key_offset = (
        jnp.arange(key_span, dtype=jnp.int32)[None, :]
        - jnp.arange(local_frames, dtype=jnp.int32)[:, None]
    )
    allowed = (
        (key_offset >= 0)
        & (key_offset <= 2 * window_half)
        & (query_seg[:, None] == key_seg[None, :])
    )
    query_heads = query_rows.reshape(local_frames, HEADS_W, head_size)
    key_heads = kv_ext[:, :head_width].reshape(key_span, HEADS_W, head_size)
    value_heads = kv_ext[:, head_width:].reshape(key_span, HEADS_W, head_size)
    scores = jnp.einsum(
        "qhe,khe->hqk", query_heads, key_heads, preferred_element_type=jnp.float32
    ) / math.sqrt(head_size)
    scores = jnp.where(allowed[None], scores, masked_score)
    row_max = jnp.max(scores, axis=2, keepdims=True)
    exp_scores = jnp.exp(scores - row_max)
    attn_probs = (exp_scores / jnp.sum(exp_scores, axis=2, keepdims=True)).astype(jnp.bfloat16)
    context = jnp.einsum(
        "hqk,khe->qhe", attn_probs, value_heads, preferred_element_type=jnp.float32
    )
    context = context.reshape(local_frames, head_width).astype(jnp.bfloat16)
    residual = (
        input_rows.astype(jnp.float32)
        + jnp.dot(context, full_weight, preferred_element_type=jnp.float32)
    ).astype(jnp.bfloat16)
    stacked_rims = with_halo(jnp.stack([residual, cotangent_rows]), ((TM, 1),), conv_reach)
    residual_ext = stacked_rims[0]
    cotangent_ext = stacked_rims[1][conv_lead : conv_lead + conv_span]
    residual_positions = (
        first_frame - conv_reach + jnp.arange(local_frames + 2 * conv_reach, dtype=jnp.int32)
    )
    residual_seg = segment_ids(starts_row, residual_positions)
    conv_seg = residual_seg[conv_lead : conv_lead + conv_span]
    own_seg = residual_seg[conv_reach : conv_reach + local_frames]
    kernel_float = full_kernel.astype(jnp.float32)
    conv_out = jnp.zeros((conv_span, residual.shape[1]), jnp.float32)
    for offset in range(KW):
        same_utt = (conv_seg == residual_seg[offset : offset + conv_span])[:, None]
        conv_out = conv_out + jnp.where(
            same_utt,
            kernel_float[offset] * residual_ext[offset : offset + conv_span].astype(jnp.float32),
            0.0,
        )
    gate_sig = jax.nn.sigmoid(conv_out)
    gated_grad = cotangent_ext.astype(jnp.float32) * gate_sig * (1.0 + conv_out * (1.0 - gate_sig))
    back_sum = cotangent_rows.astype(jnp.float32)
    own_lower = conv_lead - 1
    own_grad = gated_grad[own_lower : own_lower + local_frames]
    own_conv_seg = conv_seg[own_lower : own_lower + local_frames]
    for offset in range(KW):
        lower = KW - 1 - offset
        same_back = (conv_seg[lower : lower + local_frames] == own_seg)[:, None]
        back_sum = back_sum + jnp.where(
            same_back, kernel_float[offset] * gated_grad[lower : lower + local_frames], 0.0
        )
    products = jnp.stack(
        [
            jnp.where(
                (
                    own_conv_seg
                    == residual_seg[own_lower + offset : own_lower + offset + local_frames]
                )[:, None],
                own_grad
                * residual_ext[own_lower + offset : own_lower + offset + local_frames].astype(
                    jnp.float32
                ),
                0.0,
            )
            for offset in range(KW)
        ]
    )
    kernel_part = jnp.sum(products, axis=1)
    residual_grad = back_sum.astype(jnp.bfloat16)
    context_grad = lax.dot_general(
        residual_grad, full_weight, (((1,), (1,)), ((), ())), preferred_element_type=jnp.float32
    ).astype(jnp.bfloat16)
    grad_scale = 1.0 / math.sqrt(lax.axis_size(FSDP) * queries.shape[0] * frames_total)
    weight_part = lax.dot_general(
        context, residual_grad, (((0,), (0,)), ((), ())), preferred_element_type=jnp.float32
    )
    fsdp_size = lax.axis_size(FSDP)
    kernel_rows = kernel_part.reshape(KW, fsdp_size, -1).transpose(1, 0, 2)
    grad_parts = jnp.concatenate(
        [weight_part.reshape(fsdp_size, -1), kernel_rows.reshape(fsdp_size, -1)], axis=1
    ) * grad_scale
    grad_share = join_over_core(reduce_over_tm(halve_over_fsdp(halve_over_core(grad_parts))), 0)
    weight_size = weight_part.size // fsdp_size
    weight_grad = grad_share[:weight_size].reshape(-1, weight_part.shape[1])
    kernel_grad = grad_share[weight_size:].reshape(KW, -1)
    return (context_grad[None], weight_grad, kernel_grad)


def solution(mesh):
    tm_size, fsdp_size = mesh.shape["tm"], mesh.shape["fsdp"]
    sub_mesh = Mesh(
        mesh.devices.reshape(tm_size // 8, 4, 2, fsdp_size // 2, 2), TM_AXES + FSDP_AXES
    )
    return jax.shard_map(
        shards,
        mesh=sub_mesh,
        in_specs=(
            P(FSDP, TM, None),
            P(FSDP, TM, None),
            P(FSDP, TM, None),
            P(FSDP, TM, None),
            P(FSDP, None),
            P(None, FSDP),
            P(FSDP, None),
        ),
        out_specs=(P(FSDP, TM, None), P(FSDP, None), P(None, FSDP)),
        check_vma=False,
    )
```

```python
import math

import jax
import jax.numpy as jnp
from jax import lax
from jax.sharding import Mesh, PartitionSpec as P

HEADS_W = 8
KW = 32
WIN = 128


masked_score = -1e30

TM_AXES = ("z", "y_hi", "core")
FSDP_AXES = ("x", "y_lo")
TM = TM_AXES
FSDP = FSDP_AXES
CORE = "core"


def halve_over_fsdp(parts):
    size = parts.shape[0]
    own = lax.axis_index(FSDP)
    bits = [1 << k for k in range(size.bit_length() - 1)]
    acc = parts.reshape((2,) * len(bits) + parts.shape[1:])
    for depth, bit in enumerate(bits):
        axis = len(bits) - 1 - depth
        mine = (own & bit) != 0
        low = lax.index_in_dim(acc, 0, axis, keepdims=False)
        high = lax.index_in_dim(acc, 1, axis, keepdims=False)
        keep = jnp.where(mine, high, low)
        send = jnp.where(mine, low, high).astype(jnp.bfloat16)
        pairs = [(i, i ^ bit) for i in range(size)]
        acc = keep + lax.ppermute(send, FSDP, pairs).astype(jnp.float32)
    return acc


def double_over_fsdp(shard):
    size = lax.axis_size(FSDP)
    own = lax.axis_index(FSDP)
    bits = [1 << k for k in range(size.bit_length() - 1)]
    acc = shard
    for bit in reversed(bits):
        pairs = [(i, i ^ bit) for i in range(size)]
        got = lax.ppermute(acc, FSDP, pairs)
        acc = jnp.where((own & bit) != 0, jnp.stack([got, acc]), jnp.stack([acc, got]))
    order = tuple(reversed(range(len(bits)))) + tuple(range(len(bits), acc.ndim))
    return acc.transpose(order).reshape((size,) + shard.shape)


def split_over_core(x, axis):
    half = x.shape[axis] // 2
    mine = lax.axis_index(CORE) != 0
    return jnp.where(
        mine, lax.slice_in_dim(x, half, 2 * half, axis=axis), lax.slice_in_dim(x, 0, half, axis=axis)
    )


def join_over_core(x, axis):
    other = lax.ppermute(x, CORE, [(0, 1), (1, 0)])
    mine = lax.axis_index(CORE) != 0
    return jnp.where(
        mine, jnp.concatenate([other, x], axis=axis), jnp.concatenate([x, other], axis=axis)
    )


def halve_over_core(parts):
    half = parts.shape[-1] // 2
    mine = lax.axis_index(CORE) != 0
    low, high = parts[..., :half], parts[..., half:]
    keep = jnp.where(mine, high, low)
    send = jnp.where(mine, low, high).astype(jnp.bfloat16)
    return keep + lax.ppermute(send, CORE, [(0, 1), (1, 0)]).astype(jnp.float32)


def reduce_over_tm(share):
    sizes = [(axis, lax.axis_size(axis)) for axis in reversed(TM_AXES) if axis != CORE]
    acc = share
    for axis, n in sizes:
        pieces = acc.reshape(n, -1).astype(jnp.bfloat16)
        acc = lax.all_to_all(pieces, axis, 0, 0, tiled=True).astype(jnp.float32).sum(axis=0)
    for axis, n in reversed(sizes):
        spread = jnp.broadcast_to(acc[None], (n,) + acc.shape)
        acc = lax.all_to_all(spread, axis, 0, 0, tiled=True).reshape(-1)
    return acc


def with_halo(x, sides, width):
    for axis, dim in sides:
        devices, length = (lax.axis_size(axis), x.shape[dim])
        up = [(i, (i + 1) % devices) for i in range(devices - 1)]
        down = [(j, i) for i, j in up]
        last = lax.slice_in_dim(x, length - width, length, axis=dim)
        initial = lax.slice_in_dim(x, 0, width, axis=dim)
        before = lax.ppermute(last, axis, up)
        after = lax.ppermute(initial, axis, down)
        x = jnp.concatenate([before, x, after], axis=dim)
    return x


def segment_ids(starts_row, positions):
    return jnp.sum((starts_row[None, :] <= positions[:, None]).astype(jnp.int32), axis=1) - 1


def shards(queries, keys_values, inputs, cotangent, out_weight, conv_kernel, utt_starts):
    query_rows = queries[0]
    kv_rows = keys_values[0]
    input_rows = inputs[0]
    cotangent_rows = cotangent[0]
    starts_row = utt_starts[0]
    local_frames = query_rows.shape[0]
    head_width = query_rows.shape[1]
    head_size = head_width // HEADS_W
    window_half = WIN // 2
    conv_reach = KW - 1
    conv_lead = KW // 2
    conv_span = local_frames + KW - 1
    frames_total = local_frames * lax.axis_size(TM)
    first_frame = lax.axis_index(TM) * local_frames
    weight_rows, kernel_cols = out_weight.shape[0], conv_kernel.shape[1]
    gathered = join_over_core(
        double_over_fsdp(
            split_over_core(
                jnp.concatenate([out_weight, conv_kernel.reshape(-1, out_weight.shape[1])]), 1
            )
        ),
        2,
    )
    full_weight = gathered[:, :weight_rows].reshape(-1, out_weight.shape[1])
    full_kernel = (
        gathered[:, weight_rows:].reshape(-1, KW, kernel_cols).transpose(1, 0, 2).reshape(KW, -1)
    )
    kv_ext = with_halo(kv_rows, ((TM, 0),), window_half)
    key_span = local_frames + 2 * window_half
    key_positions = first_frame - window_half + jnp.arange(key_span, dtype=jnp.int32)
    key_seg = jnp.where(key_positions < frames_total, segment_ids(starts_row, key_positions), -1)
    query_seg = segment_ids(starts_row, first_frame + jnp.arange(local_frames, dtype=jnp.int32))
    key_offset = (
        jnp.arange(key_span, dtype=jnp.int32)[None, :]
        - jnp.arange(local_frames, dtype=jnp.int32)[:, None]
    )
    allowed = (
        (key_offset >= 0)
        & (key_offset <= 2 * window_half)
        & (query_seg[:, None] == key_seg[None, :])
    )
    query_heads = query_rows.reshape(local_frames, HEADS_W, head_size)
    key_heads = kv_ext[:, :head_width].reshape(key_span, HEADS_W, head_size)
    value_heads = kv_ext[:, head_width:].reshape(key_span, HEADS_W, head_size)
    scores = jnp.einsum(
        "qhe,khe->hqk", query_heads, key_heads, preferred_element_type=jnp.float32
    ) / math.sqrt(head_size)
    scores = jnp.where(allowed[None], scores, masked_score)
    row_max = jnp.max(scores, axis=2, keepdims=True)
    exp_scores = jnp.exp(scores - row_max)
    attn_probs = (exp_scores / jnp.sum(exp_scores, axis=2, keepdims=True)).astype(jnp.bfloat16)
    context = jnp.einsum(
        "hqk,khe->qhe", attn_probs, value_heads, preferred_element_type=jnp.float32
    )
    context = context.reshape(local_frames, head_width).astype(jnp.bfloat16)
    residual = (
        input_rows.astype(jnp.float32)
        + jnp.dot(context, full_weight, preferred_element_type=jnp.float32)
    ).astype(jnp.bfloat16)
    stacked_rims = with_halo(jnp.stack([residual, cotangent_rows]), ((TM, 1),), conv_reach)
    residual_ext = stacked_rims[0]
    cotangent_ext = stacked_rims[1][conv_lead : conv_lead + conv_span]
    residual_positions = (
        first_frame - conv_reach + jnp.arange(local_frames + 2 * conv_reach, dtype=jnp.int32)
    )
    residual_seg = segment_ids(starts_row, residual_positions)
    conv_seg = residual_seg[conv_lead : conv_lead + conv_span]
    own_seg = residual_seg[conv_reach : conv_reach + local_frames]
    kernel_float = full_kernel.astype(jnp.float32)
    conv_out = jnp.zeros((conv_span, residual.shape[1]), jnp.float32)
    for offset in range(KW):
        same_utt = (conv_seg == residual_seg[offset : offset + conv_span])[:, None]
        conv_out = conv_out + jnp.where(
            same_utt,
            kernel_float[offset] * residual_ext[offset : offset + conv_span].astype(jnp.float32),
            0.0,
        )
    gate_sig = jax.nn.sigmoid(conv_out)
    gated_grad = cotangent_ext.astype(jnp.float32) * gate_sig * (1.0 + conv_out * (1.0 - gate_sig))
    back_sum = cotangent_rows.astype(jnp.float32)
    own_lower = conv_lead - 1
    own_grad = gated_grad[own_lower : own_lower + local_frames]
    own_conv_seg = conv_seg[own_lower : own_lower + local_frames]
    for offset in range(KW):
        lower = KW - 1 - offset
        same_back = (conv_seg[lower : lower + local_frames] == own_seg)[:, None]
        back_sum = back_sum + jnp.where(
            same_back, kernel_float[offset] * gated_grad[lower : lower + local_frames], 0.0
        )
    kernel_part = jnp.stack(
        [
            jnp.where(
                (
                    own_conv_seg
                    == residual_seg[own_lower + offset : own_lower + offset + local_frames]
                )[:, None],
                own_grad
                * residual_ext[own_lower + offset : own_lower + offset + local_frames].astype(
                    jnp.float32
                ),
                0.0,
            ).sum(axis=0)
            for offset in range(KW)
        ]
    )
    residual_grad = back_sum.astype(jnp.bfloat16)
    context_grad = lax.dot_general(
        residual_grad, full_weight, (((1,), (1,)), ((), ())), preferred_element_type=jnp.float32
    ).astype(jnp.bfloat16)
    grad_scale = 1.0 / math.sqrt(lax.axis_size(FSDP) * queries.shape[0] * frames_total)
    weight_part = lax.dot_general(
        context, residual_grad, (((0,), (0,)), ((), ())), preferred_element_type=jnp.float32
    )
    fsdp_size = lax.axis_size(FSDP)
    kernel_rows = kernel_part.reshape(KW, fsdp_size, -1).transpose(1, 0, 2)
    grad_parts = jnp.concatenate(
        [weight_part.reshape(fsdp_size, -1), kernel_rows.reshape(fsdp_size, -1)], axis=1
    ) * grad_scale
    grad_share = join_over_core(reduce_over_tm(halve_over_fsdp(halve_over_core(grad_parts))), 0)
    weight_size = weight_part.size // fsdp_size
    weight_grad = grad_share[:weight_size].reshape(-1, weight_part.shape[1])
    kernel_grad = grad_share[weight_size:].reshape(KW, -1)
    return (context_grad[None], weight_grad, kernel_grad)


def solution(mesh):
    tm_size, fsdp_size = mesh.shape["tm"], mesh.shape["fsdp"]
    sub_mesh = Mesh(
        mesh.devices.reshape(tm_size // 8, 4, 2, fsdp_size // 2, 2), TM_AXES + FSDP_AXES
    )
    return jax.shard_map(
        shards,
        mesh=sub_mesh,
        in_specs=(
            P(FSDP, TM, None),
            P(FSDP, TM, None),
            P(FSDP, TM, None),
            P(FSDP, TM, None),
            P(FSDP, None),
            P(None, FSDP),
            P(FSDP, None),
        ),
        out_specs=(P(FSDP, TM, None), P(FSDP, None), P(None, FSDP)),
        check_vma=False,
    )
```

```python
import math

import jax
import jax.numpy as jnp
from jax import lax
from jax.sharding import Mesh, PartitionSpec as P

HEADS_W = 8
KW = 32
WIN = 128


masked_score = -1e30

TM_AXES = ("z", "y_hi", "core")
FSDP_AXES = ("x", "y_lo")
TM = TM_AXES
FSDP = FSDP_AXES
CORE = "core"


def halve_over_fsdp(parts):
    size = parts.shape[0]
    own = lax.axis_index(FSDP)
    bits = [1 << k for k in range(size.bit_length() - 1)]
    acc = parts.reshape((2,) * len(bits) + parts.shape[1:])
    for depth, bit in enumerate(bits):
        axis = len(bits) - 1 - depth
        mine = (own & bit) != 0
        low = lax.index_in_dim(acc, 0, axis, keepdims=False)
        high = lax.index_in_dim(acc, 1, axis, keepdims=False)
        keep = jnp.where(mine, high, low)
        send = jnp.where(mine, low, high).astype(jnp.bfloat16)
        pairs = [(i, i ^ bit) for i in range(size)]
        acc = keep + lax.ppermute(send, FSDP, pairs).astype(jnp.float32)
    return acc


def double_over_fsdp(shard):
    size = lax.axis_size(FSDP)
    own = lax.axis_index(FSDP)
    bits = [1 << k for k in range(size.bit_length() - 1)]
    acc = shard
    for bit in reversed(bits):
        pairs = [(i, i ^ bit) for i in range(size)]
        got = lax.ppermute(acc, FSDP, pairs)
        acc = jnp.where((own & bit) != 0, jnp.stack([got, acc]), jnp.stack([acc, got]))
    order = tuple(reversed(range(len(bits)))) + tuple(range(len(bits), acc.ndim))
    return acc.transpose(order).reshape((size,) + shard.shape)


def split_over_core(x, axis):
    half = x.shape[axis] // 2
    mine = lax.axis_index(CORE) != 0
    return jnp.where(
        mine, lax.slice_in_dim(x, half, 2 * half, axis=axis), lax.slice_in_dim(x, 0, half, axis=axis)
    )


def join_over_core(x, axis):
    other = lax.ppermute(x, CORE, [(0, 1), (1, 0)])
    mine = lax.axis_index(CORE) != 0
    return jnp.where(
        mine, jnp.concatenate([other, x], axis=axis), jnp.concatenate([x, other], axis=axis)
    )


def halve_over_core(parts):
    half = parts.shape[-1] // 2
    mine = lax.axis_index(CORE) != 0
    low, high = parts[..., :half], parts[..., half:]
    keep = jnp.where(mine, high, low)
    send = jnp.where(mine, low, high).astype(jnp.bfloat16)
    return keep + lax.ppermute(send, CORE, [(0, 1), (1, 0)]).astype(jnp.float32)


def reduce_over_tm(share):
    sizes = [(axis, lax.axis_size(axis)) for axis in reversed(TM_AXES) if axis != CORE]
    acc = share
    for axis, n in sizes:
        pieces = acc.reshape(n, -1).astype(jnp.bfloat16)
        acc = lax.all_to_all(pieces, axis, 0, 0, tiled=True).astype(jnp.float32).sum(axis=0)
    for axis, n in reversed(sizes):
        spread = jnp.broadcast_to(acc[None], (n,) + acc.shape)
        acc = lax.all_to_all(spread, axis, 0, 0, tiled=True).reshape(-1)
    return acc


def with_halo(x, sides, width):
    for axis, dim in sides:
        devices, length = (lax.axis_size(axis), x.shape[dim])
        up = [(i, (i + 1) % devices) for i in range(devices - 1)]
        down = [(j, i) for i, j in up]
        last = lax.slice_in_dim(x, length - width, length, axis=dim)
        initial = lax.slice_in_dim(x, 0, width, axis=dim)
        before = lax.ppermute(last, axis, up)
        after = lax.ppermute(initial, axis, down)
        x = jnp.concatenate([before, x, after], axis=dim)
    return x


def segment_ids(starts_row, positions):
    return jnp.sum((starts_row[None, :] <= positions[:, None]).astype(jnp.int32), axis=1) - 1


def shards(queries, keys_values, inputs, cotangent, out_weight, conv_kernel, utt_starts):
    query_rows = queries[0]
    kv_rows = keys_values[0]
    input_rows = inputs[0]
    cotangent_rows = cotangent[0]
    starts_row = utt_starts[0]
    local_frames = query_rows.shape[0]
    head_width = query_rows.shape[1]
    head_size = head_width // HEADS_W
    window_half = WIN // 2
    conv_reach = KW - 1
    conv_lead = KW // 2
    conv_span = local_frames + KW - 1
    frames_total = local_frames * lax.axis_size(TM)
    first_frame = lax.axis_index(TM) * local_frames
    weight_rows, kernel_cols = out_weight.shape[0], conv_kernel.shape[1]
    gathered = join_over_core(
        double_over_fsdp(
            split_over_core(
                jnp.concatenate([out_weight, conv_kernel.reshape(-1, out_weight.shape[1])]), 1
            )
        ),
        2,
    )
    full_weight = gathered[:, :weight_rows].reshape(-1, out_weight.shape[1])
    full_kernel = (
        gathered[:, weight_rows:].reshape(-1, KW, kernel_cols).transpose(1, 0, 2).reshape(KW, -1)
    )
    kv_ext = with_halo(kv_rows, ((TM, 0),), window_half)
    key_span = local_frames + 2 * window_half
    key_positions = first_frame - window_half + jnp.arange(key_span, dtype=jnp.int32)
    key_seg = jnp.where(key_positions < frames_total, segment_ids(starts_row, key_positions), -1)
    query_seg = segment_ids(starts_row, first_frame + jnp.arange(local_frames, dtype=jnp.int32))
    key_offset = (
        jnp.arange(key_span, dtype=jnp.int32)[None, :]
        - jnp.arange(local_frames, dtype=jnp.int32)[:, None]
    )
    allowed = (
        (key_offset >= 0)
        & (key_offset <= 2 * window_half)
        & (query_seg[:, None] == key_seg[None, :])
    )
    query_heads = query_rows.reshape(local_frames, HEADS_W, head_size)
    key_heads = kv_ext[:, :head_width].reshape(key_span, HEADS_W, head_size)
    value_heads = kv_ext[:, head_width:].reshape(key_span, HEADS_W, head_size)
    scores = jnp.einsum(
        "qhe,khe->hqk", query_heads, key_heads, preferred_element_type=jnp.float32
    ) / math.sqrt(head_size)
    scores = jnp.where(allowed[None], scores, masked_score)
    row_max = jnp.max(scores, axis=2, keepdims=True)
    exp_scores = jnp.exp(scores - row_max)
    attn_probs = (exp_scores / jnp.sum(exp_scores, axis=2, keepdims=True)).astype(jnp.bfloat16)
    context = jnp.einsum(
        "hqk,khe->qhe", attn_probs, value_heads, preferred_element_type=jnp.float32
    )
    context = context.reshape(local_frames, head_width).astype(jnp.bfloat16)
    residual = (
        input_rows.astype(jnp.float32)
        + jnp.dot(context, full_weight, preferred_element_type=jnp.float32)
    ).astype(jnp.bfloat16)
    stacked_rims = with_halo(jnp.stack([residual, cotangent_rows]), ((TM, 1),), conv_reach)
    residual_ext = stacked_rims[0]
    cotangent_ext = stacked_rims[1][conv_lead : conv_lead + conv_span]
    residual_positions = (
        first_frame - conv_reach + jnp.arange(local_frames + 2 * conv_reach, dtype=jnp.int32)
    )
    residual_seg = segment_ids(starts_row, residual_positions)
    conv_seg = residual_seg[conv_lead : conv_lead + conv_span]
    own_seg = residual_seg[conv_reach : conv_reach + local_frames]
    kernel_float = full_kernel.astype(jnp.float32)
    conv_out = jnp.zeros((conv_span, residual.shape[1]), jnp.float32)
    for offset in range(KW):
        same_utt = (conv_seg == residual_seg[offset : offset + conv_span])[:, None]
        conv_out = conv_out + jnp.where(
            same_utt,
            kernel_float[offset] * residual_ext[offset : offset + conv_span].astype(jnp.float32),
            0.0,
        )
    gate_sig = jax.nn.sigmoid(conv_out)
    gated_grad = cotangent_ext.astype(jnp.float32) * gate_sig * (1.0 + conv_out * (1.0 - gate_sig))
    back_sum = cotangent_rows.astype(jnp.float32)
    own_lower = conv_lead - 1
    own_grad = gated_grad[own_lower : own_lower + local_frames]
    own_conv_seg = conv_seg[own_lower : own_lower + local_frames]
    for offset in range(KW):
        lower = KW - 1 - offset
        same_back = (conv_seg[lower : lower + local_frames] == own_seg)[:, None]
        back_sum = back_sum + jnp.where(
            same_back, kernel_float[offset] * gated_grad[lower : lower + local_frames], 0.0
        )
    kernel_part = jnp.stack(
        [
            jnp.where(
                (
                    own_conv_seg
                    == residual_seg[own_lower + offset : own_lower + offset + local_frames]
                )[:, None],
                own_grad
                * residual_ext[own_lower + offset : own_lower + offset + local_frames].astype(
                    jnp.float32
                ),
                0.0,
            ).sum(axis=0)
            for offset in range(KW)
        ]
    )
    residual_grad = back_sum.astype(jnp.bfloat16)
    context_grad = lax.dot_general(
        residual_grad, full_weight, (((1,), (1,)), ((), ())), preferred_element_type=jnp.float32
    ).astype(jnp.bfloat16)
    grad_scale = 1.0 / math.sqrt(lax.axis_size(FSDP) * queries.shape[0] * frames_total)
    weight_part = lax.dot_general(
        context, residual_grad, (((0,), (0,)), ((), ())), preferred_element_type=jnp.float32
    )
    fsdp_size = lax.axis_size(FSDP)
    width = weight_part.shape[1]
    kernel_rows = kernel_part.reshape(KW, fsdp_size, -1).transpose(1, 0, 2)
    grad_parts = jnp.concatenate(
        [weight_part.reshape(fsdp_size, -1, width), kernel_rows.reshape(fsdp_size, -1, width)],
        axis=1,
    ) * grad_scale
    share = halve_over_fsdp(halve_over_core(grad_parts))
    grad_share = join_over_core(reduce_over_tm(share.reshape(-1)).reshape(share.shape), 1)
    weight_rows_own = weight_part.shape[0] // fsdp_size
    weight_grad = grad_share[:weight_rows_own]
    kernel_grad = grad_share[weight_rows_own:].reshape(KW, -1)
    return (context_grad[None], weight_grad, kernel_grad)


def solution(mesh):
    tm_size, fsdp_size = mesh.shape["tm"], mesh.shape["fsdp"]
    sub_mesh = Mesh(
        mesh.devices.reshape(tm_size // 8, 4, 2, fsdp_size // 2, 2), TM_AXES + FSDP_AXES
    )
    return jax.shard_map(
        shards,
        mesh=sub_mesh,
        in_specs=(
            P(FSDP, TM, None),
            P(FSDP, TM, None),
            P(FSDP, TM, None),
            P(FSDP, TM, None),
            P(FSDP, None),
            P(None, FSDP),
            P(FSDP, None),
        ),
        out_specs=(P(FSDP, TM, None), P(FSDP, None), P(None, FSDP)),
        check_vma=False,
    )
```

```python
import math

import jax
import jax.numpy as jnp
from jax import lax
from jax.sharding import Mesh, PartitionSpec as P

HEADS_W = 8
KW = 32
WIN = 128


masked_score = -1e30

TM_AXES = ("z", "y_hi", "core")
FSDP_AXES = ("x", "y_lo")
TM = TM_AXES
FSDP = FSDP_AXES
CORE = "core"


def halve_over_fsdp(parts):
    size = parts.shape[0]
    own = lax.axis_index(FSDP)
    bits = [1 << k for k in range(size.bit_length() - 1)]
    acc = parts.reshape((2,) * len(bits) + parts.shape[1:])
    for depth, bit in enumerate(bits):
        axis = len(bits) - 1 - depth
        mine = (own & bit) != 0
        low = lax.index_in_dim(acc, 0, axis, keepdims=False)
        high = lax.index_in_dim(acc, 1, axis, keepdims=False)
        keep = jnp.where(mine, high, low)
        send = jnp.where(mine, low, high).astype(jnp.bfloat16)
        pairs = [(i, i ^ bit) for i in range(size)]
        acc = keep + lax.ppermute(send, FSDP, pairs).astype(jnp.float32)
    return acc


def double_over_fsdp(shard, held):
    size = lax.axis_size(FSDP)
    own = lax.axis_index(FSDP)
    bits = [1 << k for k in range(size.bit_length() - 1)]
    acc = shard
    for step, bit in enumerate(reversed(bits)):
        if step == 1:
            acc, held = lax.optimization_barrier((acc, held))
        pairs = [(i, i ^ bit) for i in range(size)]
        got = lax.ppermute(acc, FSDP, pairs)
        acc = jnp.where((own & bit) != 0, jnp.stack([got, acc]), jnp.stack([acc, got]))
    order = tuple(reversed(range(len(bits)))) + tuple(range(len(bits), acc.ndim))
    return acc.transpose(order).reshape((size,) + shard.shape), held


def split_over_core(x, axis):
    half = x.shape[axis] // 2
    mine = lax.axis_index(CORE) != 0
    return jnp.where(
        mine, lax.slice_in_dim(x, half, 2 * half, axis=axis), lax.slice_in_dim(x, 0, half, axis=axis)
    )


def join_over_core(x, axis):
    other = lax.ppermute(x, CORE, [(0, 1), (1, 0)])
    mine = lax.axis_index(CORE) != 0
    return jnp.where(
        mine, jnp.concatenate([other, x], axis=axis), jnp.concatenate([x, other], axis=axis)
    )


def halve_over_core(parts):
    half = parts.shape[-1] // 2
    mine = lax.axis_index(CORE) != 0
    low, high = parts[..., :half], parts[..., half:]
    keep = jnp.where(mine, high, low)
    send = jnp.where(mine, low, high).astype(jnp.bfloat16)
    return keep + lax.ppermute(send, CORE, [(0, 1), (1, 0)]).astype(jnp.float32)


def reduce_over_tm(share):
    sizes = [(axis, lax.axis_size(axis)) for axis in reversed(TM_AXES) if axis != CORE]
    acc = share
    for axis, n in sizes:
        pieces = acc.reshape(n, -1).astype(jnp.bfloat16)
        acc = lax.all_to_all(pieces, axis, 0, 0, tiled=True).astype(jnp.float32).sum(axis=0)
    for axis, n in reversed(sizes):
        spread = jnp.broadcast_to(acc[None], (n,) + acc.shape)
        acc = lax.all_to_all(spread, axis, 0, 0, tiled=True).reshape(-1)
    return acc


def with_halo(x, sides, width):
    for axis, dim in sides:
        devices, length = (lax.axis_size(axis), x.shape[dim])
        up = [(i, (i + 1) % devices) for i in range(devices - 1)]
        down = [(j, i) for i, j in up]
        last = lax.slice_in_dim(x, length - width, length, axis=dim)
        initial = lax.slice_in_dim(x, 0, width, axis=dim)
        before = lax.ppermute(last, axis, up)
        after = lax.ppermute(initial, axis, down)
        x = jnp.concatenate([before, x, after], axis=dim)
    return x


def segment_ids(starts_row, positions):
    return jnp.sum((starts_row[None, :] <= positions[:, None]).astype(jnp.int32), axis=1) - 1


def shards(queries, keys_values, inputs, cotangent, out_weight, conv_kernel, utt_starts):
    query_rows = queries[0]
    kv_rows = keys_values[0]
    input_rows = inputs[0]
    cotangent_rows = cotangent[0]
    starts_row = utt_starts[0]
    local_frames = query_rows.shape[0]
    head_width = query_rows.shape[1]
    head_size = head_width // HEADS_W
    window_half = WIN // 2
    conv_reach = KW - 1
    conv_lead = KW // 2
    conv_span = local_frames + KW - 1
    frames_total = local_frames * lax.axis_size(TM)
    first_frame = lax.axis_index(TM) * local_frames
    kv_ext = with_halo(kv_rows, ((TM, 0),), window_half)
    key_span = local_frames + 2 * window_half
    key_positions = first_frame - window_half + jnp.arange(key_span, dtype=jnp.int32)
    key_seg = jnp.where(key_positions < frames_total, segment_ids(starts_row, key_positions), -1)
    query_seg = segment_ids(starts_row, first_frame + jnp.arange(local_frames, dtype=jnp.int32))
    key_offset = (
        jnp.arange(key_span, dtype=jnp.int32)[None, :]
        - jnp.arange(local_frames, dtype=jnp.int32)[:, None]
    )
    allowed = (
        (key_offset >= 0)
        & (key_offset <= 2 * window_half)
        & (query_seg[:, None] == key_seg[None, :])
    )
    query_heads = query_rows.reshape(local_frames, HEADS_W, head_size)
    key_heads = kv_ext[:, :head_width].reshape(key_span, HEADS_W, head_size)
    value_heads = kv_ext[:, head_width:].reshape(key_span, HEADS_W, head_size)
    scores = jnp.einsum(
        "qhe,khe->hqk", query_heads, key_heads, preferred_element_type=jnp.float32
    ) / math.sqrt(head_size)
    scores = jnp.where(allowed[None], scores, masked_score)
    row_max = jnp.max(scores, axis=2, keepdims=True)
    exp_scores = jnp.exp(scores - row_max)
    attn_probs = (exp_scores / jnp.sum(exp_scores, axis=2, keepdims=True)).astype(jnp.bfloat16)
    context = jnp.einsum(
        "hqk,khe->qhe", attn_probs, value_heads, preferred_element_type=jnp.float32
    )
    context = context.reshape(local_frames, head_width).astype(jnp.bfloat16)
    weight_rows, kernel_cols = out_weight.shape[0], conv_kernel.shape[1]
    gathered_half, context = double_over_fsdp(
        split_over_core(
            jnp.concatenate([out_weight, conv_kernel.reshape(-1, out_weight.shape[1])]), 1
        ),
        context,
    )
    gathered = join_over_core(gathered_half, 2)
    full_weight = gathered[:, :weight_rows].reshape(-1, out_weight.shape[1])
    full_kernel = (
        gathered[:, weight_rows:].reshape(-1, KW, kernel_cols).transpose(1, 0, 2).reshape(KW, -1)
    )
    residual = (
        input_rows.astype(jnp.float32)
        + jnp.dot(context, full_weight, preferred_element_type=jnp.float32)
    ).astype(jnp.bfloat16)
    stacked_rims = with_halo(jnp.stack([residual, cotangent_rows]), ((TM, 1),), conv_reach)
    residual_ext = stacked_rims[0]
    cotangent_ext = stacked_rims[1][conv_lead : conv_lead + conv_span]
    residual_positions = (
        first_frame - conv_reach + jnp.arange(local_frames + 2 * conv_reach, dtype=jnp.int32)
    )
    residual_seg = segment_ids(starts_row, residual_positions)
    conv_seg = residual_seg[conv_lead : conv_lead + conv_span]
    own_seg = residual_seg[conv_reach : conv_reach + local_frames]
    kernel_float = full_kernel.astype(jnp.float32)
    conv_out = jnp.zeros((conv_span, residual.shape[1]), jnp.float32)
    for offset in range(KW):
        same_utt = (conv_seg == residual_seg[offset : offset + conv_span])[:, None]
        conv_out = conv_out + jnp.where(
            same_utt,
            kernel_float[offset] * residual_ext[offset : offset + conv_span].astype(jnp.float32),
            0.0,
        )
    gate_sig = jax.nn.sigmoid(conv_out)
    gated_grad = cotangent_ext.astype(jnp.float32) * gate_sig * (1.0 + conv_out * (1.0 - gate_sig))
    back_sum = cotangent_rows.astype(jnp.float32)
    own_lower = conv_lead - 1
    own_grad = gated_grad[own_lower : own_lower + local_frames]
    own_conv_seg = conv_seg[own_lower : own_lower + local_frames]
    for offset in range(KW):
        lower = KW - 1 - offset
        same_back = (conv_seg[lower : lower + local_frames] == own_seg)[:, None]
        back_sum = back_sum + jnp.where(
            same_back, kernel_float[offset] * gated_grad[lower : lower + local_frames], 0.0
        )
    kernel_part = jnp.stack(
        [
            jnp.where(
                (
                    own_conv_seg
                    == residual_seg[own_lower + offset : own_lower + offset + local_frames]
                )[:, None],
                own_grad
                * residual_ext[own_lower + offset : own_lower + offset + local_frames].astype(
                    jnp.float32
                ),
                0.0,
            ).sum(axis=0)
            for offset in range(KW)
        ]
    )
    residual_grad = back_sum.astype(jnp.bfloat16)
    context_grad = lax.dot_general(
        residual_grad, full_weight, (((1,), (1,)), ((), ())), preferred_element_type=jnp.float32
    ).astype(jnp.bfloat16)
    grad_scale = 1.0 / math.sqrt(lax.axis_size(FSDP) * queries.shape[0] * frames_total)
    weight_part = lax.dot_general(
        context, residual_grad, (((0,), (0,)), ((), ())), preferred_element_type=jnp.float32
    )
    fsdp_size = lax.axis_size(FSDP)
    width = weight_part.shape[1]
    kernel_rows = kernel_part.reshape(KW, fsdp_size, -1).transpose(1, 0, 2)
    grad_parts = jnp.concatenate(
        [weight_part.reshape(fsdp_size, -1, width), kernel_rows.reshape(fsdp_size, -1, width)],
        axis=1,
    ) * grad_scale
    share = halve_over_fsdp(halve_over_core(grad_parts))
    grad_share = join_over_core(reduce_over_tm(share.reshape(-1)).reshape(share.shape), 1)
    weight_rows_own = weight_part.shape[0] // fsdp_size
    weight_grad = grad_share[:weight_rows_own]
    kernel_grad = grad_share[weight_rows_own:].reshape(KW, -1)
    return (context_grad[None], weight_grad, kernel_grad)


def solution(mesh):
    tm_size, fsdp_size = mesh.shape["tm"], mesh.shape["fsdp"]
    sub_mesh = Mesh(
        mesh.devices.reshape(tm_size // 8, 4, 2, fsdp_size // 2, 2), TM_AXES + FSDP_AXES
    )
    return jax.shard_map(
        shards,
        mesh=sub_mesh,
        in_specs=(
            P(FSDP, TM, None),
            P(FSDP, TM, None),
            P(FSDP, TM, None),
            P(FSDP, TM, None),
            P(FSDP, None),
            P(None, FSDP),
            P(FSDP, None),
        ),
        out_specs=(P(FSDP, TM, None), P(FSDP, None), P(None, FSDP)),
        check_vma=False,
    )
```

```python
import math

import jax
import jax.numpy as jnp
from jax import lax
from jax.sharding import Mesh, PartitionSpec as P

HEADS_W = 8
KW = 32
WIN = 128


masked_score = -1e30

TM_AXES = ("z", "y_hi", "core")
FSDP_AXES = ("x", "y_lo")
TM = TM_AXES
FSDP = FSDP_AXES
CORE = "core"


def halve_over_fsdp(parts):
    size = parts.shape[0]
    own = lax.axis_index(FSDP)
    bits = [1 << k for k in range(size.bit_length() - 1)]
    acc = parts.reshape((2,) * len(bits) + parts.shape[1:])
    for depth, bit in enumerate(bits):
        axis = len(bits) - 1 - depth
        mine = (own & bit) != 0
        low = lax.index_in_dim(acc, 0, axis, keepdims=False)
        high = lax.index_in_dim(acc, 1, axis, keepdims=False)
        keep = jnp.where(mine, high, low)
        send = jnp.where(mine, low, high).astype(jnp.bfloat16)
        pairs = [(i, i ^ bit) for i in range(size)]
        acc = keep + lax.ppermute(send, FSDP, pairs).astype(jnp.float32)
    return acc


def double_over_fsdp(shard, held):
    size = lax.axis_size(FSDP)
    own = lax.axis_index(FSDP)
    bits = [1 << k for k in range(size.bit_length() - 1)]
    acc = shard
    for step, bit in enumerate(reversed(bits)):
        if step == 1:
            acc, held = lax.optimization_barrier((acc, held))
        pairs = [(i, i ^ bit) for i in range(size)]
        got = lax.ppermute(acc, FSDP, pairs)
        acc = jnp.where((own & bit) != 0, jnp.stack([got, acc]), jnp.stack([acc, got]))
    order = tuple(reversed(range(len(bits)))) + tuple(range(len(bits), acc.ndim))
    return acc.transpose(order).reshape((size,) + shard.shape), held


def split_over_core(x, axis):
    half = x.shape[axis] // 2
    mine = lax.axis_index(CORE) != 0
    return jnp.where(
        mine, lax.slice_in_dim(x, half, 2 * half, axis=axis), lax.slice_in_dim(x, 0, half, axis=axis)
    )


def join_over_core(x, axis):
    other = lax.ppermute(x, CORE, [(0, 1), (1, 0)])
    mine = lax.axis_index(CORE) != 0
    return jnp.where(
        mine, jnp.concatenate([other, x], axis=axis), jnp.concatenate([x, other], axis=axis)
    )


def halve_over_core(parts):
    half = parts.shape[-1] // 2
    mine = lax.axis_index(CORE) != 0
    low, high = parts[..., :half], parts[..., half:]
    keep = jnp.where(mine, high, low)
    send = jnp.where(mine, low, high).astype(jnp.bfloat16)
    return keep + lax.ppermute(send, CORE, [(0, 1), (1, 0)]).astype(jnp.float32)


def reduce_over_tm(share):
    sizes = [(axis, lax.axis_size(axis)) for axis in reversed(TM_AXES) if axis != CORE]
    acc = share
    for axis, n in sizes:
        pieces = acc.reshape(n, -1).astype(jnp.bfloat16)
        acc = lax.all_to_all(pieces, axis, 0, 0, tiled=True).astype(jnp.float32).sum(axis=0)
    acc = acc.astype(jnp.bfloat16)
    for axis, n in reversed(sizes):
        spread = jnp.broadcast_to(acc[None], (n,) + acc.shape)
        acc = lax.all_to_all(spread, axis, 0, 0, tiled=True).reshape(-1)
    return acc


def with_halo(x, sides, width):
    for axis, dim in sides:
        devices, length = (lax.axis_size(axis), x.shape[dim])
        up = [(i, (i + 1) % devices) for i in range(devices - 1)]
        down = [(j, i) for i, j in up]
        last = lax.slice_in_dim(x, length - width, length, axis=dim)
        initial = lax.slice_in_dim(x, 0, width, axis=dim)
        before = lax.ppermute(last, axis, up)
        after = lax.ppermute(initial, axis, down)
        x = jnp.concatenate([before, x, after], axis=dim)
    return x


def segment_ids(starts_row, positions):
    return jnp.sum((starts_row[None, :] <= positions[:, None]).astype(jnp.int32), axis=1) - 1


def shards(queries, keys_values, inputs, cotangent, out_weight, conv_kernel, utt_starts):
    query_rows = queries[0]
    kv_rows = keys_values[0]
    input_rows = inputs[0]
    cotangent_rows = cotangent[0]
    starts_row = utt_starts[0]
    local_frames = query_rows.shape[0]
    head_width = query_rows.shape[1]
    head_size = head_width // HEADS_W
    window_half = WIN // 2
    conv_reach = KW - 1
    conv_lead = KW // 2
    conv_span = local_frames + KW - 1
    frames_total = local_frames * lax.axis_size(TM)
    first_frame = lax.axis_index(TM) * local_frames
    kv_ext = with_halo(kv_rows, ((TM, 0),), window_half)
    key_span = local_frames + 2 * window_half
    key_positions = first_frame - window_half + jnp.arange(key_span, dtype=jnp.int32)
    key_seg = jnp.where(key_positions < frames_total, segment_ids(starts_row, key_positions), -1)
    query_seg = segment_ids(starts_row, first_frame + jnp.arange(local_frames, dtype=jnp.int32))
    key_offset = (
        jnp.arange(key_span, dtype=jnp.int32)[None, :]
        - jnp.arange(local_frames, dtype=jnp.int32)[:, None]
    )
    allowed = (
        (key_offset >= 0)
        & (key_offset <= 2 * window_half)
        & (query_seg[:, None] == key_seg[None, :])
    )
    query_heads = query_rows.reshape(local_frames, HEADS_W, head_size)
    key_heads = kv_ext[:, :head_width].reshape(key_span, HEADS_W, head_size)
    value_heads = kv_ext[:, head_width:].reshape(key_span, HEADS_W, head_size)
    scores = jnp.einsum(
        "qhe,khe->hqk", query_heads, key_heads, preferred_element_type=jnp.float32
    ) / math.sqrt(head_size)
    scores = jnp.where(allowed[None], scores, masked_score)
    row_max = jnp.max(scores, axis=2, keepdims=True)
    exp_scores = jnp.exp(scores - row_max)
    attn_probs = (exp_scores / jnp.sum(exp_scores, axis=2, keepdims=True)).astype(jnp.bfloat16)
    context = jnp.einsum(
        "hqk,khe->qhe", attn_probs, value_heads, preferred_element_type=jnp.float32
    )
    context = context.reshape(local_frames, head_width).astype(jnp.bfloat16)
    weight_rows, kernel_cols = out_weight.shape[0], conv_kernel.shape[1]
    gathered_half, context = double_over_fsdp(
        split_over_core(
            jnp.concatenate([out_weight, conv_kernel.reshape(-1, out_weight.shape[1])]), 1
        ),
        context,
    )
    gathered = join_over_core(gathered_half, 2)
    full_weight = gathered[:, :weight_rows].reshape(-1, out_weight.shape[1])
    full_kernel = (
        gathered[:, weight_rows:].reshape(-1, KW, kernel_cols).transpose(1, 0, 2).reshape(KW, -1)
    )
    residual = (
        input_rows.astype(jnp.float32)
        + jnp.dot(context, full_weight, preferred_element_type=jnp.float32)
    ).astype(jnp.bfloat16)
    stacked_rims = with_halo(jnp.stack([residual, cotangent_rows]), ((TM, 1),), conv_reach)
    residual_ext = stacked_rims[0]
    cotangent_ext = stacked_rims[1][conv_lead : conv_lead + conv_span]
    residual_positions = (
        first_frame - conv_reach + jnp.arange(local_frames + 2 * conv_reach, dtype=jnp.int32)
    )
    residual_seg = segment_ids(starts_row, residual_positions)
    conv_seg = residual_seg[conv_lead : conv_lead + conv_span]
    own_seg = residual_seg[conv_reach : conv_reach + local_frames]
    kernel_float = full_kernel.astype(jnp.float32)
    conv_out = jnp.zeros((conv_span, residual.shape[1]), jnp.float32)
    for offset in range(KW):
        same_utt = (conv_seg == residual_seg[offset : offset + conv_span])[:, None]
        conv_out = conv_out + jnp.where(
            same_utt,
            kernel_float[offset] * residual_ext[offset : offset + conv_span].astype(jnp.float32),
            0.0,
        )
    gate_sig = jax.nn.sigmoid(conv_out)
    gated_grad = cotangent_ext.astype(jnp.float32) * gate_sig * (1.0 + conv_out * (1.0 - gate_sig))
    back_sum = cotangent_rows.astype(jnp.float32)
    own_lower = conv_lead - 1
    own_grad = gated_grad[own_lower : own_lower + local_frames]
    own_conv_seg = conv_seg[own_lower : own_lower + local_frames]
    for offset in range(KW):
        lower = KW - 1 - offset
        same_back = (conv_seg[lower : lower + local_frames] == own_seg)[:, None]
        back_sum = back_sum + jnp.where(
            same_back, kernel_float[offset] * gated_grad[lower : lower + local_frames], 0.0
        )
    kernel_part = jnp.stack(
        [
            jnp.where(
                (
                    own_conv_seg
                    == residual_seg[own_lower + offset : own_lower + offset + local_frames]
                )[:, None],
                own_grad
                * residual_ext[own_lower + offset : own_lower + offset + local_frames].astype(
                    jnp.float32
                ),
                0.0,
            ).sum(axis=0)
            for offset in range(KW)
        ]
    )
    residual_grad = back_sum.astype(jnp.bfloat16)
    context_grad = lax.dot_general(
        residual_grad, full_weight, (((1,), (1,)), ((), ())), preferred_element_type=jnp.float32
    ).astype(jnp.bfloat16)
    grad_scale = 1.0 / math.sqrt(lax.axis_size(FSDP) * queries.shape[0] * frames_total)
    weight_part = lax.dot_general(
        context, residual_grad, (((0,), (0,)), ((), ())), preferred_element_type=jnp.float32
    )
    fsdp_size = lax.axis_size(FSDP)
    width = weight_part.shape[1]
    kernel_rows = kernel_part.reshape(KW, fsdp_size, -1).transpose(1, 0, 2)
    grad_parts = jnp.concatenate(
        [weight_part.reshape(fsdp_size, -1, width), kernel_rows.reshape(fsdp_size, -1, width)],
        axis=1,
    ) * grad_scale
    share = halve_over_fsdp(halve_over_core(grad_parts))
    grad_share = join_over_core(reduce_over_tm(share.reshape(-1)).reshape(share.shape), 1).astype(
        jnp.float32
    )
    weight_rows_own = weight_part.shape[0] // fsdp_size
    weight_grad = grad_share[:weight_rows_own]
    kernel_grad = grad_share[weight_rows_own:].reshape(KW, -1)
    return (context_grad[None], weight_grad, kernel_grad)


def solution(mesh):
    tm_size, fsdp_size = mesh.shape["tm"], mesh.shape["fsdp"]
    sub_mesh = Mesh(
        mesh.devices.reshape(tm_size // 8, 4, 2, fsdp_size // 2, 2), TM_AXES + FSDP_AXES
    )
    return jax.shard_map(
        shards,
        mesh=sub_mesh,
        in_specs=(
            P(FSDP, TM, None),
            P(FSDP, TM, None),
            P(FSDP, TM, None),
            P(FSDP, TM, None),
            P(FSDP, None),
            P(None, FSDP),
            P(FSDP, None),
        ),
        out_specs=(P(FSDP, TM, None), P(FSDP, None), P(None, FSDP)),
        check_vma=False,
    )
```

```python
import math

import jax
import jax.numpy as jnp
from jax import lax
from jax.sharding import Mesh, PartitionSpec as P

HEADS_W = 8
KW = 32
WIN = 128


masked_score = -1e30

TM_AXES = ("z", "y_hi", "core")
FSDP_AXES = ("x", "y_lo")
TM = TM_AXES
FSDP = FSDP_AXES
CORE = "core"


def halve_over_fsdp(parts):
    size = parts.shape[0]
    own = lax.axis_index(FSDP)
    bits = [1 << k for k in range(size.bit_length() - 1)]
    acc = parts.reshape((2,) * len(bits) + parts.shape[1:])
    for depth, bit in enumerate(bits):
        axis = len(bits) - 1 - depth
        mine = (own & bit) != 0
        low = lax.index_in_dim(acc, 0, axis, keepdims=False)
        high = lax.index_in_dim(acc, 1, axis, keepdims=False)
        keep = jnp.where(mine, high, low)
        send = jnp.where(mine, low, high).astype(jnp.bfloat16)
        pairs = [(i, i ^ bit) for i in range(size)]
        acc = keep + lax.ppermute(send, FSDP, pairs).astype(jnp.float32)
    return acc


def double_over_fsdp(shard, held):
    size = lax.axis_size(FSDP)
    own = lax.axis_index(FSDP)
    bits = [1 << k for k in range(size.bit_length() - 1)]
    acc = shard
    for step, bit in enumerate(reversed(bits)):
        if step == 1:
            acc, held = lax.optimization_barrier((acc, held))
        pairs = [(i, i ^ bit) for i in range(size)]
        got = lax.ppermute(acc, FSDP, pairs)
        acc = jnp.where((own & bit) != 0, jnp.stack([got, acc]), jnp.stack([acc, got]))
    order = tuple(reversed(range(len(bits)))) + tuple(range(len(bits), acc.ndim))
    return acc.transpose(order).reshape((size,) + shard.shape), held


def split_over_core(x, axis):
    half = x.shape[axis] // 2
    mine = lax.axis_index(CORE) != 0
    return jnp.where(
        mine, lax.slice_in_dim(x, half, 2 * half, axis=axis), lax.slice_in_dim(x, 0, half, axis=axis)
    )


def join_over_core(x, axis):
    other = lax.ppermute(x, CORE, [(0, 1), (1, 0)])
    mine = lax.axis_index(CORE) != 0
    return jnp.where(
        mine, jnp.concatenate([other, x], axis=axis), jnp.concatenate([x, other], axis=axis)
    )


def halve_over_core(parts):
    half = parts.shape[-1] // 2
    mine = lax.axis_index(CORE) != 0
    low, high = parts[..., :half], parts[..., half:]
    keep = jnp.where(mine, high, low)
    send = jnp.where(mine, low, high).astype(jnp.bfloat16)
    return keep + lax.ppermute(send, CORE, [(0, 1), (1, 0)]).astype(jnp.float32)


def reduce_over_tm(share):
    sizes = [(axis, lax.axis_size(axis)) for axis in TM_AXES if axis != CORE]
    acc = share
    for axis, n in sizes:
        pieces = acc.reshape(n, -1).astype(jnp.bfloat16)
        acc = lax.all_to_all(pieces, axis, 0, 0, tiled=True).astype(jnp.float32).sum(axis=0)
    for axis, n in reversed(sizes):
        spread = jnp.broadcast_to(acc[None], (n,) + acc.shape)
        acc = lax.all_to_all(spread, axis, 0, 0, tiled=True).reshape(-1)
    return acc


def with_halo(x, sides, width):
    for axis, dim in sides:
        devices, length = (lax.axis_size(axis), x.shape[dim])
        up = [(i, (i + 1) % devices) for i in range(devices - 1)]
        down = [(j, i) for i, j in up]
        last = lax.slice_in_dim(x, length - width, length, axis=dim)
        initial = lax.slice_in_dim(x, 0, width, axis=dim)
        before = lax.ppermute(last, axis, up)
        after = lax.ppermute(initial, axis, down)
        x = jnp.concatenate([before, x, after], axis=dim)
    return x


def segment_ids(starts_row, positions):
    return jnp.sum((starts_row[None, :] <= positions[:, None]).astype(jnp.int32), axis=1) - 1


def shards(queries, keys_values, inputs, cotangent, out_weight, conv_kernel, utt_starts):
    query_rows = queries[0]
    kv_rows = keys_values[0]
    input_rows = inputs[0]
    cotangent_rows = cotangent[0]
    starts_row = utt_starts[0]
    local_frames = query_rows.shape[0]
    head_width = query_rows.shape[1]
    head_size = head_width // HEADS_W
    window_half = WIN // 2
    conv_reach = KW - 1
    conv_lead = KW // 2
    conv_span = local_frames + KW - 1
    frames_total = local_frames * lax.axis_size(TM)
    first_frame = lax.axis_index(TM) * local_frames
    kv_ext = with_halo(kv_rows, ((TM, 0),), window_half)
    key_span = local_frames + 2 * window_half
    key_positions = first_frame - window_half + jnp.arange(key_span, dtype=jnp.int32)
    key_seg = jnp.where(key_positions < frames_total, segment_ids(starts_row, key_positions), -1)
    query_seg = segment_ids(starts_row, first_frame + jnp.arange(local_frames, dtype=jnp.int32))
    key_offset = (
        jnp.arange(key_span, dtype=jnp.int32)[None, :]
        - jnp.arange(local_frames, dtype=jnp.int32)[:, None]
    )
    allowed = (
        (key_offset >= 0)
        & (key_offset <= 2 * window_half)
        & (query_seg[:, None] == key_seg[None, :])
    )
    query_heads = query_rows.reshape(local_frames, HEADS_W, head_size)
    key_heads = kv_ext[:, :head_width].reshape(key_span, HEADS_W, head_size)
    value_heads = kv_ext[:, head_width:].reshape(key_span, HEADS_W, head_size)
    scores = jnp.einsum(
        "qhe,khe->hqk", query_heads, key_heads, preferred_element_type=jnp.float32
    ) / math.sqrt(head_size)
    scores = jnp.where(allowed[None], scores, masked_score)
    row_max = jnp.max(scores, axis=2, keepdims=True)
    exp_scores = jnp.exp(scores - row_max)
    attn_probs = (exp_scores / jnp.sum(exp_scores, axis=2, keepdims=True)).astype(jnp.bfloat16)
    context = jnp.einsum(
        "hqk,khe->qhe", attn_probs, value_heads, preferred_element_type=jnp.float32
    )
    context = context.reshape(local_frames, head_width).astype(jnp.bfloat16)
    weight_rows, kernel_cols = out_weight.shape[0], conv_kernel.shape[1]
    gathered_half, context = double_over_fsdp(
        split_over_core(
            jnp.concatenate([out_weight, conv_kernel.reshape(-1, out_weight.shape[1])]), 1
        ),
        context,
    )
    gathered = join_over_core(gathered_half, 2)
    full_weight = gathered[:, :weight_rows].reshape(-1, out_weight.shape[1])
    full_kernel = (
        gathered[:, weight_rows:].reshape(-1, KW, kernel_cols).transpose(1, 0, 2).reshape(KW, -1)
    )
    residual = (
        input_rows.astype(jnp.float32)
        + jnp.dot(context, full_weight, preferred_element_type=jnp.float32)
    ).astype(jnp.bfloat16)
    stacked_rims = with_halo(jnp.stack([residual, cotangent_rows]), ((TM, 1),), conv_reach)
    residual_ext = stacked_rims[0]
    cotangent_ext = stacked_rims[1][conv_lead : conv_lead + conv_span]
    residual_positions = (
        first_frame - conv_reach + jnp.arange(local_frames + 2 * conv_reach, dtype=jnp.int32)
    )
    residual_seg = segment_ids(starts_row, residual_positions)
    conv_seg = residual_seg[conv_lead : conv_lead + conv_span]
    own_seg = residual_seg[conv_reach : conv_reach + local_frames]
    kernel_float = full_kernel.astype(jnp.float32)
    conv_out = jnp.zeros((conv_span, residual.shape[1]), jnp.float32)
    for offset in range(KW):
        same_utt = (conv_seg == residual_seg[offset : offset + conv_span])[:, None]
        conv_out = conv_out + jnp.where(
            same_utt,
            kernel_float[offset] * residual_ext[offset : offset + conv_span].astype(jnp.float32),
            0.0,
        )
    gate_sig = jax.nn.sigmoid(conv_out)
    gated_grad = cotangent_ext.astype(jnp.float32) * gate_sig * (1.0 + conv_out * (1.0 - gate_sig))
    back_sum = cotangent_rows.astype(jnp.float32)
    own_lower = conv_lead - 1
    own_grad = gated_grad[own_lower : own_lower + local_frames]
    own_conv_seg = conv_seg[own_lower : own_lower + local_frames]
    for offset in range(KW):
        lower = KW - 1 - offset
        same_back = (conv_seg[lower : lower + local_frames] == own_seg)[:, None]
        back_sum = back_sum + jnp.where(
            same_back, kernel_float[offset] * gated_grad[lower : lower + local_frames], 0.0
        )
    kernel_part = jnp.stack(
        [
            jnp.where(
                (
                    own_conv_seg
                    == residual_seg[own_lower + offset : own_lower + offset + local_frames]
                )[:, None],
                own_grad
                * residual_ext[own_lower + offset : own_lower + offset + local_frames].astype(
                    jnp.float32
                ),
                0.0,
            ).sum(axis=0)
            for offset in range(KW)
        ]
    )
    residual_grad = back_sum.astype(jnp.bfloat16)
    context_grad = lax.dot_general(
        residual_grad, full_weight, (((1,), (1,)), ((), ())), preferred_element_type=jnp.float32
    ).astype(jnp.bfloat16)
    grad_scale = 1.0 / math.sqrt(lax.axis_size(FSDP) * queries.shape[0] * frames_total)
    weight_part = lax.dot_general(
        context, residual_grad, (((0,), (0,)), ((), ())), preferred_element_type=jnp.float32
    )
    fsdp_size = lax.axis_size(FSDP)
    width = weight_part.shape[1]
    kernel_rows = kernel_part.reshape(KW, fsdp_size, -1).transpose(1, 0, 2)
    grad_parts = jnp.concatenate(
        [weight_part.reshape(fsdp_size, -1, width), kernel_rows.reshape(fsdp_size, -1, width)],
        axis=1,
    ) * grad_scale
    share = halve_over_fsdp(halve_over_core(grad_parts))
    grad_share = join_over_core(reduce_over_tm(share.reshape(-1)).reshape(share.shape), 1)
    weight_rows_own = weight_part.shape[0] // fsdp_size
    weight_grad = grad_share[:weight_rows_own]
    kernel_grad = grad_share[weight_rows_own:].reshape(KW, -1)
    return (context_grad[None], weight_grad, kernel_grad)


def solution(mesh):
    tm_size, fsdp_size = mesh.shape["tm"], mesh.shape["fsdp"]
    sub_mesh = Mesh(
        mesh.devices.reshape(tm_size // 8, 4, 2, fsdp_size // 2, 2), TM_AXES + FSDP_AXES
    )
    return jax.shard_map(
        shards,
        mesh=sub_mesh,
        in_specs=(
            P(FSDP, TM, None),
            P(FSDP, TM, None),
            P(FSDP, TM, None),
            P(FSDP, TM, None),
            P(FSDP, None),
            P(None, FSDP),
            P(FSDP, None),
        ),
        out_specs=(P(FSDP, TM, None), P(FSDP, None), P(None, FSDP)),
        check_vma=False,
    )
```
